256 devices in a mesh: gx: 32 (over z, y_lo, core), gy: 8 (over y_hi, x).
Axes of the slice: x: 4, y: 4 (y_hi: 2, y_lo: 2; y = y_hi * 2 + y_lo), z: 8, core: 2. Of those that a mesh axis runs over, the one named last changes fastest.
Arguments:
- state: bfloat16 [4, 2, 4096, 4096], P(None, None, 'gx', 'gy'), may hold values from -6 to 6
- heights: int32 [4096, 4096], P('gx', 'gy'), may hold values from 0 to 1
- surface_flag: int32 [4096, 4096], P('gx', 'gy'), may hold values 0 or 1
Outputs:
- tendency: bfloat16 [4, 2, 4096, 4096], P(None, None, 'gx', 'gy')
- spectrum: float32 [2, 2, 4096, 4096], P(None, None, ('gx', 'gy'))
The draws below stay inside these ranges and needn't reach their ends.
All inputs are finite; a program needn't handle non-finite values. No bound on the sum of `surface_flag` on one device may be relied on, other than what follows from the above.
Results may differ from the reference program's by a relative error of at most 0.002.
Values may be sent and summed in bfloat16 or wider, within the bound.
No kernel may reach another device: no remote copies, remote signals or barrier semaphores. Data moves between devices by JAX's collectives and lax.ppermute only.
A program may use at most 64 MiB of HBM per device.

```python
import jax
import jax.numpy as jnp
from jax import lax

NX = 4096
NY = 4096
NZ = 2


def with_ends(values, own_key, smallest, top_value):
    longest = values.shape.index(max(values.shape))
    spots = []
    for shift in (0, 1):
        where = [jax.random.randint(jax.random.fold_in(own_key, axis), (), 0, length) for axis, length in enumerate(values.shape)]
        where[longest] = (where[longest] + shift) % values.shape[longest]
        spots.append(tuple(where))
    return values.at[spots[0]].set(smallest).at[spots[1]].set(top_value)


def level_of(key, shape, cuts, smallest, top_value):
    loudness = 1.0
    for position, parts in cuts:
        steps = jax.random.uniform(jax.random.fold_in(jax.random.fold_in(key, 6), position), (parts,), jnp.float32, smallest / len(cuts), top_value / len(cuts))
        loudness = loudness * jnp.repeat(jnp.exp(steps), shape[position] // parts).reshape((-1,) + (1,) * (len(shape) - 1 - position))
    return loudness


def gaussian(stream_key, extent, scale, bound, split=(), kind=jnp.bfloat16):
    loudness = level_of(stream_key, extent, split, -0.22, 0.18) if split else 1.0
    values = jax.random.normal(stream_key, extent, jnp.float32) * scale * loudness
    return jnp.minimum(jnp.maximum(values, -bound), bound).astype(kind)


def setup_inputs(seed: int = 0) -> dict:
    key_list = jax.random.split(jax.random.key(seed), 4)
    state = gaussian(key_list[0], (4, NZ, NX, NY), 1.0, 6.0, ((2, 32), (3, 8)))
    heights = with_ends(jax.random.randint(key_list[1], (NX, NY), 0, NZ // 2 + 1), jax.random.fold_in(key_list[1], 1), 0, (NZ // 2 + 1) - 1).astype(jnp.int32)
    surface_flag = with_ends((jax.random.randint(key_list[2], (NX, NY), 0, 2) < 1).astype(jnp.int32), jax.random.fold_in(key_list[2], 1), 0, 1)
    return {"state": state, "heights": heights, "surface_flag": surface_flag}


NU = 0.1
BETA = 0.5
HEAT = 1.0
DT = 0.5


def raised(field):
    zero = jnp.zeros_like(field[:1])
    return jnp.concatenate([field[1:], zero], axis=0)


def lowered(field):
    zero = jnp.zeros_like(field[:1])
    return jnp.concatenate([zero, field[:-1]], axis=0)


def tendency_one(component, field, pick, center, fluid, surface):
    slope_x = (45.0 * (pick(1, 0) - pick(-1, 0)) - 9.0 * (pick(2, 0) - pick(-2, 0)) + (pick(3, 0) - pick(-3, 0))) / 60.0
    slope_y = (45.0 * (pick(0, 1) - pick(0, -1)) - 9.0 * (pick(0, 2) - pick(0, -2)) + (pick(0, 3) - pick(0, -3))) / 60.0
    above = raised(field)
    below = lowered(field)
    slope_z = (above - below) * 0.5
    advect = center[0] * slope_x + center[1] * slope_y + center[2] * slope_z
    spread = (pick(1, 0) + pick(-1, 0) + pick(0, 1) + pick(0, -1) - 4.0 * field) + (above + below - 2.0 * field)
    result = NU * spread - advect
    if component == 2:
        result = result + BETA * center[3]
    if component == 3:
        result = result + HEAT * surface
    return fluid * result


def reference(state, heights, surface_flag):
    level = lax.broadcasted_iota(jnp.int32, state.shape[1:], 0)
    fluid = (level >= heights[None]).astype(jnp.float32)
    surface = (level == heights[None]).astype(jnp.float32) * surface_flag[None].astype(jnp.float32)
    masked = state.astype(jnp.float32) * fluid[None]
    pieces = []
    for component in range(4):
        field = masked[component]

        def pick(step_x, step_y, field=field):
            return jnp.roll(field, (-step_x, -step_y), axis=(1, 2))

        pieces.append(tendency_one(component, field, pick, masked, fluid, surface).astype(jnp.bfloat16))
    tendency = jnp.stack(pieces)
    star = masked[:3] + DT * tendency[:3].astype(jnp.float32)
    diverge = ((jnp.roll(star[0], -1, 1) - jnp.roll(star[0], 1, 1)) + (jnp.roll(star[1], -1, 2) - jnp.roll(star[1], 1, 2)) + (raised(star[2]) - lowered(star[2]))) * 0.5
    transformed = jnp.fft.fft2(diverge, axes=(1, 2), norm="ortho")
    transformed = jnp.transpose(transformed, (0, 2, 1))
    spectrum = jnp.stack([jnp.real(transformed), jnp.imag(transformed)]).astype(jnp.float32)
    return tendency, spectrum
```

```python
import math

import numpy as np
import jax
import jax.numpy as jnp
from jax import lax
from jax.sharding import PartitionSpec as P

NU = 0.1
BETA = 0.5
HEAT = 1.0
DT = 0.5
PREC = lax.Precision.HIGH


def ring(count):
    up = [(i, (i + 1) % count) for i in range(count)]
    down = [(j, i) for i, j in up]
    return up, down


def raised(field):
    zero = jnp.zeros_like(field[:1])
    return jnp.concatenate([field[1:], zero], axis=0)


def lowered(field):
    zero = jnp.zeros_like(field[:1])
    return jnp.concatenate([zero, field[:-1]], axis=0)


def tendency_one(component, field, pick, center, fluid, surface):
    slope_x = (
        45.0 * (pick(1, 0) - pick(-1, 0))
        - 9.0 * (pick(2, 0) - pick(-2, 0))
        + (pick(3, 0) - pick(-3, 0))
    ) / 60.0
    slope_y = (
        45.0 * (pick(0, 1) - pick(0, -1))
        - 9.0 * (pick(0, 2) - pick(0, -2))
        + (pick(0, 3) - pick(0, -3))
    ) / 60.0
    above = raised(field)
    below = lowered(field)
    slope_z = (above - below) * 0.5
    advect = center[0] * slope_x + center[1] * slope_y + center[2] * slope_z
    spread = (
        pick(1, 0)
        + pick(-1, 0)
        + pick(0, 1)
        + pick(0, -1)
        - 4.0 * field
        + (above + below - 2.0 * field)
    )
    result = NU * spread - advect
    if component == 2:
        result = result + BETA * center[3]
    if component == 3:
        result = result + HEAT * surface
    return fluid * result


def cos_sin(rows, cols, length, scale=1.0):
    product = (np.arange(rows)[:, None] * np.arange(cols)[None, :]) % length
    angle = product * (2.0 * math.pi / length)
    return np.cos(angle) * scale, np.sin(angle) * scale


def const(array):
    return jnp.asarray(np.asarray(array, dtype=np.float32))


def y_tables(n_p, n_q):
    c1, s1 = cos_sin(n_p, n_p, n_p)
    w1 = np.concatenate([c1, -s1], axis=0)
    t_c, t_s = cos_sin(n_p, n_q, n_p * n_q)
    c2, s2 = cos_sin(n_q, n_q, n_q)
    w2 = np.zeros((n_q, 2, 2, n_q))
    w2[:, 0, 0] = c2
    w2[:, 0, 1] = s2
    w2[:, 1, 0] = -s2
    w2[:, 1, 1] = c2
    return w1, t_c, t_s, w2.reshape(2 * n_q, 2 * n_q)


def x_tables(n_s, n_i, scale):
    c2, s2 = cos_sin(n_s, n_s, n_s)
    wa = np.zeros((n_s, 2, 2, n_s))
    wa[:, 0, 0] = c2
    wa[:, 1, 0] = s2
    wa[:, 0, 1] = -s2
    wa[:, 1, 1] = c2
    t_c, t_s = cos_sin(n_i, n_s, n_s * n_i)
    cb, sb = cos_sin(n_i, n_i, n_i, scale)
    wb = np.zeros((2, n_i, 2, n_i))
    wb[0, :, 0] = cb
    wb[0, :, 1] = sb
    wb[1, :, 0] = -sb
    wb[1, :, 1] = cb
    return wa.reshape(2 * n_s, 2 * n_s), t_c, t_s, wb.reshape(2 * n_i, 2 * n_i)


def body(state, heights, surface_flag):
    levels = state.shape[1]
    rows_x = state.shape[2]
    rows_y = state.shape[3]
    count_x = lax.axis_size("gx")
    count_y = lax.axis_size("gy")
    up_x, down_x = ring(count_x)
    up_y, down_y = ring(count_y)

    level = lax.broadcasted_iota(jnp.int32, state.shape[1:], 0)
    fluid = (level >= heights[None]).astype(jnp.float32)
    surface = (level == heights[None]).astype(jnp.float32) * surface_flag[None].astype(jnp.float32)
    masked = state * fluid.astype(jnp.bfloat16)[None]

    x_before = lax.ppermute(masked[:, :, rows_x - 3 :, :], "gx", up_x)
    x_after = lax.ppermute(masked[:, :, :3, :], "gx", down_x)
    y_before = lax.ppermute(masked[:, :, :, rows_y - 3 :], "gy", up_y)
    y_after = lax.ppermute(masked[:, :, :, :3], "gy", down_y)
    pad_x = jnp.concatenate([x_before, masked, x_after], axis=2).astype(jnp.float32)
    pad_y = jnp.concatenate([y_before, masked, y_after], axis=3).astype(jnp.float32)
    center = masked.astype(jnp.float32)

    pieces = []
    for component in range(4):

        def pick(step_x, step_y, component=component):
            if step_y == 0:
                return pad_x[component, :, 3 + step_x : 3 + step_x + rows_x, :]
            return pad_y[component, :, :, 3 + step_y : 3 + step_y + rows_y]

        pieces.append(
            tendency_one(component, center[component], pick, center, fluid, surface).astype(
                jnp.bfloat16
            )
        )
    tendency = jnp.stack(pieces)

    star = center[:3] + DT * tendency[:3].astype(jnp.float32)
    flow_u, flow_v, flow_w = star[0], star[1], star[2]
    u_before = lax.ppermute(flow_u[:, rows_x - 1 :, :], "gx", up_x)
    u_after = lax.ppermute(flow_u[:, :1, :], "gx", down_x)
    v_before = lax.ppermute(flow_v[:, :, rows_y - 1 :], "gy", up_y)
    v_after = lax.ppermute(flow_v[:, :, :1], "gy", down_y)
    u_next = jnp.concatenate([flow_u[:, 1:, :], u_after], axis=1)
    u_prev = jnp.concatenate([u_before, flow_u[:, :-1, :]], axis=1)
    v_next = jnp.concatenate([flow_v[:, :, 1:], v_after], axis=2)
    v_prev = jnp.concatenate([v_before, flow_v[:, :, :-1]], axis=2)
    diverge = ((u_next - u_prev) + (v_next - v_prev) + (raised(flow_w) - lowered(flow_w))) * 0.5

    total_y = rows_y * count_y
    n_q = 256
    n_p = total_y // n_q
    split_y = rows_y // n_q
    piece_x = rows_x // count_y
    sent = diverge.reshape(levels, rows_x, split_y, n_q).transpose(0, 2, 1, 3)
    columns = lax.all_to_all(sent, "gy", split_axis=2, concat_axis=1, tiled=True)
    w1, t1c, t1s, w2 = y_tables(n_p, n_q)
    w1b = jnp.broadcast_to(const(w1)[None], (levels,) + w1.shape)
    stage1 = lax.dot_general(
        w1b, columns, (((2,), (1,)), ((0,), (0,))), precision=PREC
    )
    real1 = stage1[:, :n_p]
    imag1 = stage1[:, n_p:]
    tc = const(t1c)[None, :, None, :]
    ts = const(t1s)[None, :, None, :]
    real_t = real1 * tc + imag1 * ts
    imag_t = imag1 * tc - real1 * ts
    rows_m = levels * n_p * piece_x
    joined = jnp.concatenate(
        [real_t.reshape(rows_m, n_q), imag_t.reshape(rows_m, n_q)], axis=1
    )
    spectrum_y = lax.dot_general(
        const(w2), joined, (((1,), (1,)), ((), ())), precision=PREC
    )
    devices = count_x * count_y
    spectrum_y = spectrum_y.reshape(devices, 2, rows_m)
    moved = lax.all_to_all(spectrum_y, ("gx", "gy"), split_axis=0, concat_axis=0, tiled=True)

    total_x = rows_x * count_x
    n_s = devices
    n_i = piece_x
    scale = 1.0 / math.sqrt(total_x * total_y)
    wa, t2c, t2s, wb = x_tables(n_s, n_i, scale)
    stage_a = lax.dot_general(
        moved.reshape(2 * n_s, rows_m), const(wa), (((0,), (0,)), ((), ())), precision=PREC
    )
    batch = levels * n_p
    stage_a = stage_a.reshape(batch, n_i, 2 * n_s)
    real_a = stage_a[:, :, :n_s]
    imag_a = stage_a[:, :, n_s:]
    uc = const(t2c)[None]
    us = const(t2s)[None]
    real_b = real_a * uc + imag_a * us
    imag_b = imag_a * uc - real_a * us
    joined_x = jnp.concatenate([real_b, imag_b], axis=1)
    wbb = jnp.broadcast_to(const(wb)[None], (batch,) + wb.shape)
    result = lax.dot_general(
        wbb, joined_x, (((2,), (1,)), ((0,), (0,))), precision=PREC
    )
    result = result.reshape(levels, n_p, 2, n_i, n_s).transpose(2, 0, 1, 3, 4)
    spectrum = result.reshape(2, levels, n_p, total_x)
    return (tendency, spectrum)


def solution(mesh):
    return jax.shard_map(
        body,
        mesh=mesh,
        in_specs=(P(None, None, "gx", "gy"), P("gx", "gy"), P("gx", "gy")),
        out_specs=(P(None, None, "gx", "gy"), P(None, None, ("gx", "gy"), None)),
        check_vma=False,
    )
```

```python
import math

import numpy as np
import jax
import jax.numpy as jnp
from jax import lax
from jax.sharding import PartitionSpec as P

NU = 0.1
BETA = 0.5
HEAT = 1.0
DT = 0.5
PREC = lax.Precision.HIGH


def ring(count):
    up = [(i, (i + 1) % count) for i in range(count)]
    down = [(j, i) for i, j in up]
    return up, down


def raised(field):
    zero = jnp.zeros_like(field[:1])
    return jnp.concatenate([field[1:], zero], axis=0)


def lowered(field):
    zero = jnp.zeros_like(field[:1])
    return jnp.concatenate([zero, field[:-1]], axis=0)


def tendency_one(component, field, pick, center, fluid, surface):
    slope_x = (
        45.0 * (pick(1, 0) - pick(-1, 0))
        - 9.0 * (pick(2, 0) - pick(-2, 0))
        + (pick(3, 0) - pick(-3, 0))
    ) / 60.0
    slope_y = (
        45.0 * (pick(0, 1) - pick(0, -1))
        - 9.0 * (pick(0, 2) - pick(0, -2))
        + (pick(0, 3) - pick(0, -3))
    ) / 60.0
    above = raised(field)
    below = lowered(field)
    slope_z = (above - below) * 0.5
    advect = center[0] * slope_x + center[1] * slope_y + center[2] * slope_z
    spread = (
        pick(1, 0)
        + pick(-1, 0)
        + pick(0, 1)
        + pick(0, -1)
        - 4.0 * field
        + (above + below - 2.0 * field)
    )
    result = NU * spread - advect
    if component == 2:
        result = result + BETA * center[3]
    if component == 3:
        result = result + HEAT * surface
    return fluid * result


def cos_sin(rows, cols, length, scale=1.0):
    product = (np.arange(rows)[:, None] * np.arange(cols)[None, :]) % length
    angle = product * (2.0 * math.pi / length)
    return np.cos(angle) * scale, np.sin(angle) * scale


def const(array):
    return jnp.asarray(np.asarray(array, dtype=np.float32))


def y_tables(n_p, n_q):
    c1, s1 = cos_sin(n_p, n_p, n_p)
    w1 = np.concatenate([c1, -s1], axis=0)
    t_c, t_s = cos_sin(n_p, n_q, n_p * n_q)
    c2, s2 = cos_sin(n_q, n_q, n_q)
    w2 = np.zeros((n_q, 2, 2, n_q))
    w2[:, 0, 0] = c2
    w2[:, 0, 1] = s2
    w2[:, 1, 0] = -s2
    w2[:, 1, 1] = c2
    return w1, t_c, t_s, w2.reshape(2 * n_q, 2 * n_q)


def x_tables(n_s, n_i, scale):
    c2, s2 = cos_sin(n_s, n_s, n_s)
    wa = np.zeros((n_s, 2, 2, n_s))
    wa[:, 0, 0] = c2
    wa[:, 1, 0] = s2
    wa[:, 0, 1] = -s2
    wa[:, 1, 1] = c2
    t_c, t_s = cos_sin(n_i, n_s, n_s * n_i)
    cb, sb = cos_sin(n_i, n_i, n_i, scale)
    wb = np.zeros((2, n_i, 2, n_i))
    wb[0, :, 0] = cb
    wb[0, :, 1] = sb
    wb[1, :, 0] = -sb
    wb[1, :, 1] = cb
    return wa.reshape(2 * n_s, 2 * n_s), t_c, t_s, wb.reshape(2 * n_i, 2 * n_i)


def body(state, heights, surface_flag):
    levels = state.shape[1]
    rows_x = state.shape[2]
    rows_y = state.shape[3]
    count_x = lax.axis_size("gx")
    count_y = lax.axis_size("gy")
    up_x, down_x = ring(count_x)
    up_y, down_y = ring(count_y)

    level = lax.broadcasted_iota(jnp.int32, state.shape[1:], 0)
    fluid = (level >= heights[None]).astype(jnp.float32)
    surface = (level == heights[None]).astype(jnp.float32) * surface_flag[None].astype(jnp.float32)
    masked = state * fluid.astype(jnp.bfloat16)[None]

    x_before = lax.ppermute(masked[:, :, rows_x - 3 :, :], "gx", up_x)
    x_after = lax.ppermute(masked[:, :, :3, :], "gx", down_x)
    y_before = lax.ppermute(masked[:, :, :, rows_y - 3 :], "gy", up_y)
    y_after = lax.ppermute(masked[:, :, :, :3], "gy", down_y)
    pad_x = jnp.concatenate([x_before, masked, x_after], axis=2).astype(jnp.float32)
    pad_y = jnp.concatenate([y_before, masked, y_after], axis=3).astype(jnp.float32)
    center = masked.astype(jnp.float32)

    pieces = []
    for component in range(4):

        def pick(step_x, step_y, component=component):
            if step_y == 0:
                return pad_x[component, :, 3 + step_x : 3 + step_x + rows_x, :]
            return pad_y[component, :, :, 3 + step_y : 3 + step_y + rows_y]

        pieces.append(
            tendency_one(component, center[component], pick, center, fluid, surface).astype(
                jnp.bfloat16
            )
        )
    tendency = jnp.stack(pieces)

    star = center[:3] + DT * tendency[:3].astype(jnp.float32)
    flow_u, flow_v, flow_w = star[0], star[1], star[2]
    u_before = lax.ppermute(flow_u[:, rows_x - 1 :, :], "gx", up_x)
    u_after = lax.ppermute(flow_u[:, :1, :], "gx", down_x)
    v_before = lax.ppermute(flow_v[:, :, rows_y - 1 :], "gy", up_y)
    v_after = lax.ppermute(flow_v[:, :, :1], "gy", down_y)
    u_next = jnp.concatenate([flow_u[:, 1:, :], u_after], axis=1)
    u_prev = jnp.concatenate([u_before, flow_u[:, :-1, :]], axis=1)
    v_next = jnp.concatenate([flow_v[:, :, 1:], v_after], axis=2)
    v_prev = jnp.concatenate([v_before, flow_v[:, :, :-1]], axis=2)
    diverge = ((u_next - u_prev) + (v_next - v_prev) + (raised(flow_w) - lowered(flow_w))) * 0.5

    total_y = rows_y * count_y
    n_q = 256
    n_p = total_y // n_q
    split_y = rows_y // n_q
    piece_x = rows_x // count_y
    sent = diverge.reshape(levels, count_y, piece_x, split_y, n_q).transpose(1, 3, 0, 2, 4)
    sent = sent.reshape(count_y, split_y * levels * piece_x, n_q)
    columns = lax.all_to_all(sent, "gy", split_axis=0, concat_axis=0, tiled=True)
    columns = columns.reshape(n_p, levels, piece_x, n_q)
    w1, t1c, t1s, w2 = y_tables(n_p, n_q)
    stage1 = lax.dot_general(
        const(w1), columns, (((1,), (0,)), ((), ())), precision=PREC
    )
    real1 = stage1[:n_p]
    imag1 = stage1[n_p:]
    tc = const(t1c)[:, None, None, :]
    ts = const(t1s)[:, None, None, :]
    real_t = real1 * tc + imag1 * ts
    imag_t = imag1 * tc - real1 * ts
    rows_m = levels * n_p * piece_x
    joined = jnp.concatenate(
        [real_t.reshape(rows_m, n_q), imag_t.reshape(rows_m, n_q)], axis=1
    )
    devices = count_x * count_y
    spectrum_y = lax.dot_general(
        const(w2.reshape(devices, 2, 2 * n_q)), joined, (((2,), (1,)), ((), ())), precision=PREC
    )
    moved = lax.all_to_all(spectrum_y, ("gx", "gy"), split_axis=0, concat_axis=0, tiled=True)

    total_x = rows_x * count_x
    n_s = devices
    n_i = piece_x
    scale = 1.0 / math.sqrt(total_x * total_y)
    wa, t2c, t2s, wb = x_tables(n_s, n_i, scale)
    stage_a = lax.dot_general(
        moved.reshape(2 * n_s, rows_m), const(wa), (((0,), (0,)), ((), ())), precision=PREC
    )
    batch = levels * n_p
    stage_a = stage_a.reshape(batch, n_i, 2 * n_s)
    real_a = stage_a[:, :, :n_s]
    imag_a = stage_a[:, :, n_s:]
    uc = const(t2c)[None]
    us = const(t2s)[None]
    real_b = real_a * uc + imag_a * us
    imag_b = imag_a * uc - real_a * us
    joined_x = jnp.concatenate([real_b, imag_b], axis=1)
    wbb = jnp.broadcast_to(const(wb)[None], (batch,) + wb.shape)
    result = lax.dot_general(
        wbb, joined_x, (((2,), (1,)), ((0,), (0,))), precision=PREC
    )
    result = result.reshape(n_p, levels, 2, n_i, n_s).transpose(2, 1, 0, 3, 4)
    spectrum = result.reshape(2, levels, n_p, total_x)
    return (tendency, spectrum)


def solution(mesh):
    return jax.shard_map(
        body,
        mesh=mesh,
        in_specs=(P(None, None, "gx", "gy"), P("gx", "gy"), P("gx", "gy")),
        out_specs=(P(None, None, "gx", "gy"), P(None, None, ("gx", "gy"), None)),
        check_vma=False,
    )
```

```python
import math

import numpy as np
import jax
import jax.numpy as jnp
from jax import lax
from jax.sharding import PartitionSpec as P

NU = 0.1
BETA = 0.5
HEAT = 1.0
DT = 0.5
PREC = lax.Precision.HIGH


def ring(count):
    up = [(i, (i + 1) % count) for i in range(count)]
    down = [(j, i) for i, j in up]
    return up, down


def raised(field):
    zero = jnp.zeros_like(field[:1])
    return jnp.concatenate([field[1:], zero], axis=0)


def lowered(field):
    zero = jnp.zeros_like(field[:1])
    return jnp.concatenate([zero, field[:-1]], axis=0)


def tendency_one(component, field, pick, center, fluid, surface):
    slope_x = (
        45.0 * (pick(1, 0) - pick(-1, 0))
        - 9.0 * (pick(2, 0) - pick(-2, 0))
        + (pick(3, 0) - pick(-3, 0))
    ) / 60.0
    slope_y = (
        45.0 * (pick(0, 1) - pick(0, -1))
        - 9.0 * (pick(0, 2) - pick(0, -2))
        + (pick(0, 3) - pick(0, -3))
    ) / 60.0
    above = raised(field)
    below = lowered(field)
    slope_z = (above - below) * 0.5
    advect = center[0] * slope_x + center[1] * slope_y + center[2] * slope_z
    spread = (
        pick(1, 0)
        + pick(-1, 0)
        + pick(0, 1)
        + pick(0, -1)
        - 4.0 * field
        + (above + below - 2.0 * field)
    )
    result = NU * spread - advect
    if component == 2:
        result = result + BETA * center[3]
    if component == 3:
        result = result + HEAT * surface
    return fluid * result


def cos_sin(rows, cols, length, scale=1.0):
    product = (np.arange(rows)[:, None] * np.arange(cols)[None, :]) % length
    angle = product * (2.0 * math.pi / length)
    return np.cos(angle) * scale, np.sin(angle) * scale


def const(array):
    return jnp.asarray(np.asarray(array, dtype=np.float32))


def y_tables(n_p, n_q):
    c1, s1 = cos_sin(n_p, n_p, n_p)
    w1 = np.concatenate([c1, -s1], axis=0)
    t_c, t_s = cos_sin(n_p, n_q, n_p * n_q)
    c2, s2 = cos_sin(n_q, n_q, n_q)
    w2 = np.zeros((n_q, 2, 2, n_q))
    w2[:, 0, 0] = c2
    w2[:, 0, 1] = s2
    w2[:, 1, 0] = -s2
    w2[:, 1, 1] = c2
    return w1, t_c, t_s, w2.reshape(2 * n_q, 2 * n_q)


def x_tables(n_s, n_i, scale):
    c2, s2 = cos_sin(n_s, n_s, n_s)
    wa = np.zeros((n_s, 2, 2, n_s))
    wa[:, 0, 0] = c2
    wa[:, 1, 0] = s2
    wa[:, 0, 1] = -s2
    wa[:, 1, 1] = c2
    t_c, t_s = cos_sin(n_i, n_s, n_s * n_i)
    cb, sb = cos_sin(n_i, n_i, n_i, scale)
    wb = np.zeros((2, n_i, 2, n_i))
    wb[0, :, 0] = cb
    wb[0, :, 1] = sb
    wb[1, :, 0] = -sb
    wb[1, :, 1] = cb
    return wa.reshape(2 * n_s, 2 * n_s), t_c, t_s, wb.reshape(2 * n_i, 2 * n_i)


def body(state, heights, surface_flag):
    levels = state.shape[1]
    rows_x = state.shape[2]
    rows_y = state.shape[3]
    count_x = lax.axis_size("gx")
    count_y = lax.axis_size("gy")
    up_x, down_x = ring(count_x)
    up_y, down_y = ring(count_y)

    level = lax.broadcasted_iota(jnp.int32, state.shape[1:], 0)
    fluid = (level >= heights[None]).astype(jnp.float32)
    surface = (level == heights[None]).astype(jnp.float32) * surface_flag[None].astype(jnp.float32)
    masked = state * fluid.astype(jnp.bfloat16)[None]

    halo = 4
    held = jnp.concatenate([masked, fluid.astype(jnp.bfloat16)[None]], axis=0)
    lo_x, hi_x = slice(0, halo), slice(rows_x - halo, rows_x)
    lo_y, hi_y = slice(0, halo), slice(rows_y - halo, rows_y)
    x_before = lax.ppermute(held[:, :, hi_x, :], "gx", up_x)
    x_after = lax.ppermute(held[:, :, lo_x, :], "gx", down_x)
    y_before = lax.ppermute(held[:, :, :, hi_y], "gy", up_y)
    y_after = lax.ppermute(held[:, :, :, lo_y], "gy", down_y)

    def diagonal(step_x, step_y):
        return [
            (a * count_y + b, ((a + step_x) % count_x) * count_y + (b + step_y) % count_y)
            for a in range(count_x)
            for b in range(count_y)
        ]

    both = ("gx", "gy")
    corner_mm = lax.ppermute(held[:, :, hi_x, hi_y], both, diagonal(1, 1))
    corner_mp = lax.ppermute(held[:, :, hi_x, lo_y], both, diagonal(1, -1))
    corner_pm = lax.ppermute(held[:, :, lo_x, hi_y], both, diagonal(-1, 1))
    corner_pp = lax.ppermute(held[:, :, lo_x, lo_y], both, diagonal(-1, -1))
    top = jnp.concatenate([corner_mm, x_before, corner_mp], axis=3)
    middle = jnp.concatenate([y_before, held, y_after], axis=3)
    bottom = jnp.concatenate([corner_pm, x_after, corner_pp], axis=3)
    padded = jnp.concatenate([top, middle, bottom], axis=2).astype(jnp.float32)

    def region(grow):
        span_x = rows_x + 2 * grow
        span_y = rows_y + 2 * grow
        base = halo - grow
        center = padded[:4, :, base : base + span_x, base : base + span_y]
        fluid_r = padded[4, :, base : base + span_x, base : base + span_y]

        def picker(component):
            def pick(step_x, step_y):
                return padded[
                    component,
                    :,
                    base + step_x : base + step_x + span_x,
                    base + step_y : base + step_y + span_y,
                ]

            return pick

        return center, fluid_r, picker

    center_g, fluid_g, picker_g = region(1)
    center_0, fluid_0, picker_0 = region(0)
    grown = [
        tendency_one(c, center_g[c], picker_g(c), center_g, fluid_g, None).astype(jnp.bfloat16)
        for c in range(2)
    ]
    inner = [
        tendency_one(c, center_0[c], picker_0(c), center_0, fluid_0, surface).astype(jnp.bfloat16)
        for c in range(2, 4)
    ]
    tendency = jnp.stack([g[:, 1:-1, 1:-1] for g in grown] + inner)

    star_u = center_g[0] + DT * grown[0].astype(jnp.float32)
    star_v = center_g[1] + DT * grown[1].astype(jnp.float32)
    flow_w = center_0[2] + DT * inner[0].astype(jnp.float32)
    u_next = star_u[:, 2:, 1:-1]
    u_prev = star_u[:, :-2, 1:-1]
    v_next = star_v[:, 1:-1, 2:]
    v_prev = star_v[:, 1:-1, :-2]
    diverge = ((u_next - u_prev) + (v_next - v_prev) + (raised(flow_w) - lowered(flow_w))) * 0.5

    total_y = rows_y * count_y
    n_q = 256
    n_p = total_y // n_q
    split_y = rows_y // n_q
    piece_x = rows_x // count_y
    sent = diverge.reshape(levels, count_y, piece_x, split_y, n_q).transpose(1, 3, 0, 2, 4)
    sent = sent.reshape(count_y, split_y * levels * piece_x, n_q)
    columns = lax.all_to_all(sent, "gy", split_axis=0, concat_axis=0, tiled=True)
    columns = columns.reshape(n_p, levels, piece_x, n_q)
    w1, t1c, t1s, w2 = y_tables(n_p, n_q)
    stage1 = lax.dot_general(
        const(w1), columns, (((1,), (0,)), ((), ())), precision=PREC
    )
    real1 = stage1[:n_p]
    imag1 = stage1[n_p:]
    tc = const(t1c)[:, None, None, :]
    ts = const(t1s)[:, None, None, :]
    real_t = real1 * tc + imag1 * ts
    imag_t = imag1 * tc - real1 * ts
    rows_m = levels * n_p * piece_x
    joined = jnp.concatenate(
        [real_t.reshape(rows_m, n_q), imag_t.reshape(rows_m, n_q)], axis=1
    )
    devices = count_x * count_y
    spectrum_y = lax.dot_general(
        const(w2.reshape(devices, 2, 2 * n_q)), joined, (((2,), (1,)), ((), ())), precision=PREC
    )
    moved = lax.all_to_all(spectrum_y, ("gx", "gy"), split_axis=0, concat_axis=0, tiled=True)

    total_x = rows_x * count_x
    n_s = devices
    n_i = piece_x
    scale = 1.0 / math.sqrt(total_x * total_y)
    wa, t2c, t2s, wb = x_tables(n_s, n_i, scale)
    stage_a = lax.dot_general(
        moved.reshape(2 * n_s, rows_m), const(wa), (((0,), (0,)), ((), ())), precision=PREC
    )
    batch = levels * n_p
    stage_a = stage_a.reshape(batch, n_i, 2 * n_s)
    real_a = stage_a[:, :, :n_s]
    imag_a = stage_a[:, :, n_s:]
    uc = const(t2c)[None]
    us = const(t2s)[None]
    real_b = real_a * uc + imag_a * us
    imag_b = imag_a * uc - real_a * us
    joined_x = jnp.concatenate([real_b, imag_b], axis=1)
    wbb = jnp.broadcast_to(const(wb)[None], (batch,) + wb.shape)
    result = lax.dot_general(
        wbb, joined_x, (((2,), (1,)), ((0,), (0,))), precision=PREC
    )
    result = result.reshape(n_p, levels, 2, n_i, n_s).transpose(2, 1, 0, 3, 4)
    spectrum = result.reshape(2, levels, n_p, total_x)
    return (tendency, spectrum)


def solution(mesh):
    return jax.shard_map(
        body,
        mesh=mesh,
        in_specs=(P(None, None, "gx", "gy"), P("gx", "gy"), P("gx", "gy")),
        out_specs=(P(None, None, "gx", "gy"), P(None, None, ("gx", "gy"), None)),
        check_vma=False,
    )
```

```python
import math

import numpy as np
import jax
import jax.numpy as jnp
from jax import lax
from jax.sharding import PartitionSpec as P

NU = 0.1
BETA = 0.5
HEAT = 1.0
DT = 0.5
PREC = lax.Precision.HIGH


def ring(count):
    up = [(i, (i + 1) % count) for i in range(count)]
    down = [(j, i) for i, j in up]
    return up, down


def raised(field):
    zero = jnp.zeros_like(field[:1])
    return jnp.concatenate([field[1:], zero], axis=0)


def lowered(field):
    zero = jnp.zeros_like(field[:1])
    return jnp.concatenate([zero, field[:-1]], axis=0)


def tendency_one(component, field, pick, center, fluid, surface):
    slope_x = (
        45.0 * (pick(1, 0) - pick(-1, 0))
        - 9.0 * (pick(2, 0) - pick(-2, 0))
        + (pick(3, 0) - pick(-3, 0))
    ) / 60.0
    slope_y = (
        45.0 * (pick(0, 1) - pick(0, -1))
        - 9.0 * (pick(0, 2) - pick(0, -2))
        + (pick(0, 3) - pick(0, -3))
    ) / 60.0
    above = raised(field)
    below = lowered(field)
    slope_z = (above - below) * 0.5
    advect = center[0] * slope_x + center[1] * slope_y + center[2] * slope_z
    spread = (
        pick(1, 0)
        + pick(-1, 0)
        + pick(0, 1)
        + pick(0, -1)
        - 4.0 * field
        + (above + below - 2.0 * field)
    )
    result = NU * spread - advect
    if component == 2:
        result = result + BETA * center[3]
    if component == 3:
        result = result + HEAT * surface
    return fluid * result


def cos_sin(rows, cols, length, scale=1.0):
    product = (np.arange(rows)[:, None] * np.arange(cols)[None, :]) % length
    angle = product * (2.0 * math.pi / length)
    return np.cos(angle) * scale, np.sin(angle) * scale


def const(array):
    return jnp.asarray(np.asarray(array, dtype=np.float32))


def runtime_cos_sin(n, salt):
    row = lax.broadcasted_iota(jnp.int32, (n, n), 0)
    col = lax.broadcasted_iota(jnp.int32, (n, n), 1)
    product = (row * col + salt) % n
    angle = product.astype(jnp.float32) * (2.0 * math.pi / n)
    return jnp.cos(angle), jnp.sin(angle)


def y_tables(n_p, n_q):
    c1, s1 = cos_sin(n_p, n_p, n_p)
    w1 = np.concatenate([c1, -s1], axis=0)
    t_c, t_s = cos_sin(n_p, n_q, n_p * n_q)
    return w1, t_c, t_s


def x_tables(n_s, n_i, scale):
    t_c, t_s = cos_sin(n_i, n_s, n_s * n_i)
    cb, sb = cos_sin(n_i, n_i, n_i, scale)
    wb = np.zeros((2, n_i, 2, n_i))
    wb[0, :, 0] = cb
    wb[0, :, 1] = sb
    wb[1, :, 0] = -sb
    wb[1, :, 1] = cb
    return t_c, t_s, wb.reshape(2 * n_i, 2 * n_i)


def body(state, heights, surface_flag):
    levels = state.shape[1]
    rows_x = state.shape[2]
    rows_y = state.shape[3]
    count_x = lax.axis_size("gx")
    count_y = lax.axis_size("gy")
    up_x, down_x = ring(count_x)
    up_y, down_y = ring(count_y)

    level = lax.broadcasted_iota(jnp.int32, state.shape[1:], 0)
    fluid = (level >= heights[None]).astype(jnp.float32)
    surface = (level == heights[None]).astype(jnp.float32) * surface_flag[None].astype(jnp.float32)
    masked = state * fluid.astype(jnp.bfloat16)[None]

    x_before = lax.ppermute(masked[:, :, rows_x - 3 :, :], "gx", up_x)
    x_after = lax.ppermute(masked[:, :, :3, :], "gx", down_x)
    y_before = lax.ppermute(masked[:, :, :, rows_y - 3 :], "gy", up_y)
    y_after = lax.ppermute(masked[:, :, :, :3], "gy", down_y)
    pad_x = jnp.concatenate([x_before, masked, x_after], axis=2).astype(jnp.float32)
    pad_y = jnp.concatenate([y_before, masked, y_after], axis=3).astype(jnp.float32)
    center = masked.astype(jnp.float32)

    pieces = []
    for component in range(4):

        def pick(step_x, step_y, component=component):
            if step_y == 0:
                return pad_x[component, :, 3 + step_x : 3 + step_x + rows_x, :]
            return pad_y[component, :, :, 3 + step_y : 3 + step_y + rows_y]

        pieces.append(
            tendency_one(component, center[component], pick, center, fluid, surface).astype(
                jnp.bfloat16
            )
        )
    tendency = jnp.stack(pieces)

    star = center[:3] + DT * tendency[:3].astype(jnp.float32)
    flow_u, flow_v, flow_w = star[0], star[1], star[2]
    u_before = lax.ppermute(flow_u[:, rows_x - 1 :, :], "gx", up_x)
    u_after = lax.ppermute(flow_u[:, :1, :], "gx", down_x)
    v_before = lax.ppermute(flow_v[:, :, rows_y - 1 :], "gy", up_y)
    v_after = lax.ppermute(flow_v[:, :, :1], "gy", down_y)
    u_next = jnp.concatenate([flow_u[:, 1:, :], u_after], axis=1)
    u_prev = jnp.concatenate([u_before, flow_u[:, :-1, :]], axis=1)
    v_next = jnp.concatenate([flow_v[:, :, 1:], v_after], axis=2)
    v_prev = jnp.concatenate([v_before, flow_v[:, :, :-1]], axis=2)
    diverge = ((u_next - u_prev) + (v_next - v_prev) + (raised(flow_w) - lowered(flow_w))) * 0.5

    total_y = rows_y * count_y
    n_q = 256
    n_p = total_y // n_q
    split_y = rows_y // n_q
    piece_x = rows_x // count_y
    sent = diverge.reshape(levels, count_y, piece_x, split_y, n_q).transpose(1, 3, 0, 2, 4)
    sent = sent.reshape(count_y, split_y * levels * piece_x, n_q)
    columns = lax.all_to_all(sent, "gy", split_axis=0, concat_axis=0, tiled=True)
    columns = columns.reshape(n_p, levels, piece_x, n_q)
    w1, t1c, t1s = y_tables(n_p, n_q)
    devices = count_x * count_y
    salt = jnp.minimum(lax.axis_index("gx"), 0)
    big_c, big_s = runtime_cos_sin(devices, salt)
    w2 = jnp.stack([jnp.stack([big_c, big_s], axis=1), jnp.stack([-big_s, big_c], axis=1)], axis=1)
    w2 = w2.reshape(devices, 2, 2 * n_q)
    wa = jnp.stack([jnp.stack([big_c, -big_s], axis=1), jnp.stack([big_s, big_c], axis=1)], axis=1)
    wa = wa.reshape(2 * devices, 2 * devices)
    stage1 = lax.dot_general(
        const(w1), columns, (((1,), (0,)), ((), ())), precision=PREC
    )
    real1 = stage1[:n_p]
    imag1 = stage1[n_p:]
    tc = const(t1c)[:, None, None, :]
    ts = const(t1s)[:, None, None, :]
    real_t = real1 * tc + imag1 * ts
    imag_t = imag1 * tc - real1 * ts
    rows_m = levels * n_p * piece_x
    joined = jnp.concatenate(
        [real_t.reshape(rows_m, n_q), imag_t.reshape(rows_m, n_q)], axis=1
    )
    spectrum_y = lax.dot_general(
        w2, joined, (((2,), (1,)), ((), ())), precision=PREC
    )
    moved = lax.all_to_all(spectrum_y, ("gx", "gy"), split_axis=0, concat_axis=0, tiled=True)

    total_x = rows_x * count_x
    n_s = devices
    n_i = piece_x
    scale = 1.0 / math.sqrt(total_x * total_y)
    t2c, t2s, wb = x_tables(n_s, n_i, scale)
    stage_a = lax.dot_general(
        moved.reshape(2 * n_s, rows_m), wa, (((0,), (0,)), ((), ())), precision=PREC
    )
    batch = levels * n_p
    stage_a = stage_a.reshape(batch, n_i, 2 * n_s)
    real_a = stage_a[:, :, :n_s]
    imag_a = stage_a[:, :, n_s:]
    uc = const(t2c)[None]
    us = const(t2s)[None]
    real_b = real_a * uc + imag_a * us
    imag_b = imag_a * uc - real_a * us
    joined_x = jnp.concatenate([real_b, imag_b], axis=1)
    wbb = jnp.broadcast_to(const(wb)[None], (batch,) + wb.shape)
    result = lax.dot_general(
        wbb, joined_x, (((2,), (1,)), ((0,), (0,))), precision=PREC
    )
    result = result.reshape(n_p, levels, 2, n_i, n_s).transpose(2, 1, 0, 3, 4)
    spectrum = result.reshape(2, levels, n_p, total_x)
    return (tendency, spectrum)


def solution(mesh):
    return jax.shard_map(
        body,
        mesh=mesh,
        in_specs=(P(None, None, "gx", "gy"), P("gx", "gy"), P("gx", "gy")),
        out_specs=(P(None, None, "gx", "gy"), P(None, None, ("gx", "gy"), None)),
        check_vma=False,
    )
```

```python
import math

import numpy as np
import jax
import jax.numpy as jnp
from jax import lax
from jax.sharding import PartitionSpec as P

NU = 0.1
BETA = 0.5
HEAT = 1.0
DT = 0.5
PREC = lax.Precision.HIGH


def ring(count):
    up = [(i, (i + 1) % count) for i in range(count)]
    down = [(j, i) for i, j in up]
    return up, down


def raised(field):
    zero = jnp.zeros_like(field[:1])
    return jnp.concatenate([field[1:], zero], axis=0)


def lowered(field):
    zero = jnp.zeros_like(field[:1])
    return jnp.concatenate([zero, field[:-1]], axis=0)


def tendency_one(component, field, pick, center, fluid, surface):
    slope_x = (
        45.0 * (pick(1, 0) - pick(-1, 0))
        - 9.0 * (pick(2, 0) - pick(-2, 0))
        + (pick(3, 0) - pick(-3, 0))
    ) / 60.0
    slope_y = (
        45.0 * (pick(0, 1) - pick(0, -1))
        - 9.0 * (pick(0, 2) - pick(0, -2))
        + (pick(0, 3) - pick(0, -3))
    ) / 60.0
    above = raised(field)
    below = lowered(field)
    slope_z = (above - below) * 0.5
    advect = center[0] * slope_x + center[1] * slope_y + center[2] * slope_z
    spread = (
        pick(1, 0)
        + pick(-1, 0)
        + pick(0, 1)
        + pick(0, -1)
        - 4.0 * field
        + (above + below - 2.0 * field)
    )
    result = NU * spread - advect
    if component == 2:
        result = result + BETA * center[3]
    if component == 3:
        result = result + HEAT * surface
    return fluid * result


def cos_sin(rows, cols, length, scale=1.0):
    product = (np.arange(rows)[:, None] * np.arange(cols)[None, :]) % length
    angle = product * (2.0 * math.pi / length)
    return np.cos(angle) * scale, np.sin(angle) * scale


def const(array):
    return jnp.asarray(np.asarray(array, dtype=np.float32))


def y_tables(n_p, n_q):
    c1, s1 = cos_sin(n_p, n_p, n_p)
    w1 = np.concatenate([c1, -s1], axis=0)
    t_c, t_s = cos_sin(n_p, n_q, n_p * n_q)
    c2, s2 = cos_sin(n_q, n_q, n_q)
    w2 = np.zeros((n_q, 2, 2, n_q))
    w2[:, 0, 0] = c2
    w2[:, 0, 1] = s2
    w2[:, 1, 0] = -s2
    w2[:, 1, 1] = c2
    return w1, t_c, t_s, w2.reshape(2 * n_q, 2 * n_q)


def x_tables(n_s, n_i, scale):
    c2, s2 = cos_sin(n_s, n_s, n_s)
    wa = np.zeros((n_s, 2, 2, n_s))
    wa[:, 0, 0] = c2
    wa[:, 1, 0] = s2
    wa[:, 0, 1] = -s2
    wa[:, 1, 1] = c2
    t_c, t_s = cos_sin(n_i, n_s, n_s * n_i)
    cb, sb = cos_sin(n_i, n_i, n_i, scale)
    wb = np.zeros((2, n_i, 2, n_i))
    wb[0, :, 0] = cb
    wb[0, :, 1] = sb
    wb[1, :, 0] = -sb
    wb[1, :, 1] = cb
    return wa.reshape(2 * n_s, 2 * n_s), t_c, t_s, wb.reshape(2 * n_i, 2 * n_i)


def body(state, heights, surface_flag):
    levels = state.shape[1]
    rows_x = state.shape[2]
    rows_y = state.shape[3]
    count_x = lax.axis_size("gx")
    count_y = lax.axis_size("gy")
    up_x, down_x = ring(count_x)
    up_y, down_y = ring(count_y)

    level = lax.broadcasted_iota(jnp.int32, state.shape[1:], 0)
    fluid = (level >= heights[None]).astype(jnp.float32)
    surface = (level == heights[None]).astype(jnp.float32) * surface_flag[None].astype(jnp.float32)
    masked = state * fluid.astype(jnp.bfloat16)[None]

    x_before = lax.ppermute(masked[:, :, rows_x - 3 :, :], "gx", up_x)
    x_after = lax.ppermute(masked[:, :, :3, :], "gx", down_x)
    y_before = lax.ppermute(masked[:, :, :, rows_y - 3 :], "gy", up_y)
    y_after = lax.ppermute(masked[:, :, :, :3], "gy", down_y)
    pad_x = jnp.concatenate([x_before, masked, x_after], axis=2).astype(jnp.float32)
    pad_y = jnp.concatenate([y_before, masked, y_after], axis=3).astype(jnp.float32)
    center = masked.astype(jnp.float32)

    pieces = []
    for component in range(4):

        def pick(step_x, step_y, component=component):
            if step_y == 0:
                return pad_x[component, :, 3 + step_x : 3 + step_x + rows_x, :]
            return pad_y[component, :, :, 3 + step_y : 3 + step_y + rows_y]

        pieces.append(
            tendency_one(component, center[component], pick, center, fluid, surface).astype(
                jnp.bfloat16
            )
        )
    tendency = jnp.stack(pieces)

    flow_u = center[0] + DT * pieces[0].astype(jnp.float32)
    flow_v = center[1] + DT * pieces[1].astype(jnp.float32)
    flow_w = center[2] + DT * pieces[2].astype(jnp.float32)
    u_before = lax.ppermute(flow_u[:, rows_x - 1 :, :], "gx", up_x)
    u_after = lax.ppermute(flow_u[:, :1, :], "gx", down_x)
    v_before = lax.ppermute(flow_v[:, :, rows_y - 1 :], "gy", up_y)
    v_after = lax.ppermute(flow_v[:, :, :1], "gy", down_y)
    u_next = jnp.concatenate([flow_u[:, 1:, :], u_after], axis=1)
    u_prev = jnp.concatenate([u_before, flow_u[:, :-1, :]], axis=1)
    v_next = jnp.concatenate([flow_v[:, :, 1:], v_after], axis=2)
    v_prev = jnp.concatenate([v_before, flow_v[:, :, :-1]], axis=2)
    diverge = ((u_next - u_prev) + (v_next - v_prev) + (raised(flow_w) - lowered(flow_w))) * 0.5

    total_y = rows_y * count_y
    n_q = 256
    n_p = total_y // n_q
    split_y = rows_y // n_q
    piece_x = rows_x // count_y
    sent = diverge.reshape(levels, count_y, piece_x, split_y, n_q).transpose(1, 3, 0, 2, 4)
    sent = sent.reshape(count_y, split_y * levels * piece_x, n_q)
    columns = lax.all_to_all(sent, "gy", split_axis=0, concat_axis=0, tiled=True)
    columns = columns.reshape(n_p, levels, piece_x, n_q)
    w1, t1c, t1s, w2 = y_tables(n_p, n_q)
    stage1 = lax.dot_general(
        const(w1), columns, (((1,), (0,)), ((), ())), precision=PREC
    )
    real1 = stage1[:n_p]
    imag1 = stage1[n_p:]
    tc = const(t1c)[:, None, None, :]
    ts = const(t1s)[:, None, None, :]
    real_t = real1 * tc + imag1 * ts
    imag_t = imag1 * tc - real1 * ts
    rows_m = levels * n_p * piece_x
    joined = jnp.concatenate(
        [real_t.reshape(rows_m, n_q), imag_t.reshape(rows_m, n_q)], axis=1
    )
    devices = count_x * count_y
    spectrum_y = lax.dot_general(
        const(w2.reshape(devices, 2, 2 * n_q)), joined, (((2,), (1,)), ((), ())), precision=PREC
    )
    moved = lax.all_to_all(spectrum_y, ("gx", "gy"), split_axis=0, concat_axis=0, tiled=True)

    total_x = rows_x * count_x
    n_s = devices
    n_i = piece_x
    scale = 1.0 / math.sqrt(total_x * total_y)
    wa, t2c, t2s, wb = x_tables(n_s, n_i, scale)
    stage_a = lax.dot_general(
        moved.reshape(2 * n_s, rows_m), const(wa), (((0,), (0,)), ((), ())), precision=PREC
    )
    batch = levels * n_p
    stage_a = stage_a.reshape(batch, n_i, 2 * n_s)
    real_a = stage_a[:, :, :n_s]
    imag_a = stage_a[:, :, n_s:]
    uc = const(t2c)[None]
    us = const(t2s)[None]
    real_b = real_a * uc + imag_a * us
    imag_b = imag_a * uc - real_a * us
    joined_x = jnp.concatenate([real_b, imag_b], axis=1)
    wbb = jnp.broadcast_to(const(wb)[None], (batch,) + wb.shape)
    result = lax.dot_general(
        wbb, joined_x, (((2,), (1,)), ((0,), (0,))), precision=PREC
    )
    result = result.reshape(n_p, levels, 2, n_i, n_s).transpose(2, 1, 0, 3, 4)
    spectrum = result.reshape(2, levels, n_p, total_x)
    return (tendency, spectrum)


def solution(mesh):
    return jax.shard_map(
        body,
        mesh=mesh,
        in_specs=(P(None, None, "gx", "gy"), P("gx", "gy"), P("gx", "gy")),
        out_specs=(P(None, None, "gx", "gy"), P(None, None, ("gx", "gy"), None)),
        check_vma=False,
    )
```

```python
import math

import numpy as np
import jax
import jax.numpy as jnp
from jax import lax
from jax.sharding import PartitionSpec as P

NU = 0.1
BETA = 0.5
HEAT = 1.0
DT = 0.5
PREC = lax.Precision.HIGH


def ring(count):
    up = [(i, (i + 1) % count) for i in range(count)]
    down = [(j, i) for i, j in up]
    return up, down


def raised(field):
    zero = jnp.zeros_like(field[:1])
    return jnp.concatenate([field[1:], zero], axis=0)


def lowered(field):
    zero = jnp.zeros_like(field[:1])
    return jnp.concatenate([zero, field[:-1]], axis=0)


def tendency_one(component, field, pick, center, fluid, surface):
    slope_x = (
        45.0 * (pick(1, 0) - pick(-1, 0))
        - 9.0 * (pick(2, 0) - pick(-2, 0))
        + (pick(3, 0) - pick(-3, 0))
    ) / 60.0
    slope_y = (
        45.0 * (pick(0, 1) - pick(0, -1))
        - 9.0 * (pick(0, 2) - pick(0, -2))
        + (pick(0, 3) - pick(0, -3))
    ) / 60.0
    above = raised(field)
    below = lowered(field)
    slope_z = (above - below) * 0.5
    advect = center[0] * slope_x + center[1] * slope_y + center[2] * slope_z
    spread = (
        pick(1, 0)
        + pick(-1, 0)
        + pick(0, 1)
        + pick(0, -1)
        - 4.0 * field
        + (above + below - 2.0 * field)
    )
    result = NU * spread - advect
    if component == 2:
        result = result + BETA * center[3]
    if component == 3:
        result = result + HEAT * surface
    return fluid * result


def cos_sin(rows, cols, length, scale=1.0):
    product = (np.arange(rows)[:, None] * np.arange(cols)[None, :]) % length
    angle = product * (2.0 * math.pi / length)
    return np.cos(angle) * scale, np.sin(angle) * scale


def const(array):
    return jnp.asarray(np.asarray(array, dtype=np.float32))


def y_tables(n_p, n_q):
    c1, s1 = cos_sin(n_p, n_p, n_p)
    w1 = np.concatenate([c1, -s1], axis=0)
    t_c, t_s = cos_sin(n_p, n_q, n_p * n_q)
    c2, s2 = cos_sin(n_q, n_q, n_q)
    w2 = np.zeros((n_q, 2, 2, n_q))
    w2[:, 0, 0] = c2
    w2[:, 0, 1] = s2
    w2[:, 1, 0] = -s2
    w2[:, 1, 1] = c2
    return w1, t_c, t_s, w2.reshape(2 * n_q, 2 * n_q)


def x_tables(n_s, n_i, scale):
    c2, s2 = cos_sin(n_s, n_s, n_s)
    wa = np.zeros((n_s, 2, 2, n_s))
    wa[:, 0, 0] = c2
    wa[:, 1, 0] = s2
    wa[:, 0, 1] = -s2
    wa[:, 1, 1] = c2
    t_c, t_s = cos_sin(n_i, n_s, n_s * n_i)
    cb, sb = cos_sin(n_i, n_i, n_i, scale)
    wb = np.zeros((2, n_i, 2, n_i))
    wb[0, :, 0] = cb
    wb[0, :, 1] = sb
    wb[1, :, 0] = -sb
    wb[1, :, 1] = cb
    return wa.reshape(2 * n_s, 2 * n_s), t_c, t_s, wb.reshape(2 * n_i, 2 * n_i)


def body(state, heights, surface_flag):
    levels = state.shape[1]
    rows_x = state.shape[2]
    rows_y = state.shape[3]
    count_x = lax.axis_size("gx")
    count_y = lax.axis_size("gy")
    up_x, down_x = ring(count_x)
    up_y, down_y = ring(count_y)

    level = lax.broadcasted_iota(jnp.int32, state.shape[1:], 0)
    fluid = (level >= heights[None]).astype(jnp.float32)
    surface = (level == heights[None]).astype(jnp.float32) * surface_flag[None].astype(jnp.float32)
    masked = state * fluid.astype(jnp.bfloat16)[None]

    x_before = lax.ppermute(masked[:, :, rows_x - 3 :, :], "gx", up_x)
    x_after = lax.ppermute(masked[:, :, :3, :], "gx", down_x)
    y_before = lax.ppermute(masked[:, :, :, rows_y - 3 :], "gy", up_y)
    y_after = lax.ppermute(masked[:, :, :, :3], "gy", down_y)
    pad_x = jnp.concatenate([x_before, masked, x_after], axis=2).astype(jnp.float32)
    pad_y = jnp.concatenate([y_before, masked, y_after], axis=3).astype(jnp.float32)
    center = masked.astype(jnp.float32)

    pieces = []
    rounded = []
    for component in range(4):

        def pick(step_x, step_y, component=component):
            if step_y == 0:
                return pad_x[component, :, 3 + step_x : 3 + step_x + rows_x, :]
            return pad_y[component, :, :, 3 + step_y : 3 + step_y + rows_y]

        exact = tendency_one(component, center[component], pick, center, fluid, surface)
        pieces.append(exact.astype(jnp.bfloat16))
        rounded.append(lax.reduce_precision(exact, exponent_bits=8, mantissa_bits=7))
    tendency = jnp.stack(pieces)

    flow_u = center[0] + DT * rounded[0]
    flow_v = center[1] + DT * rounded[1]
    flow_w = center[2] + DT * rounded[2]
    u_before = lax.ppermute(flow_u[:, rows_x - 1 :, :], "gx", up_x)
    u_after = lax.ppermute(flow_u[:, :1, :], "gx", down_x)
    v_before = lax.ppermute(flow_v[:, :, rows_y - 1 :], "gy", up_y)
    v_after = lax.ppermute(flow_v[:, :, :1], "gy", down_y)
    u_next = jnp.concatenate([flow_u[:, 1:, :], u_after], axis=1)
    u_prev = jnp.concatenate([u_before, flow_u[:, :-1, :]], axis=1)
    v_next = jnp.concatenate([flow_v[:, :, 1:], v_after], axis=2)
    v_prev = jnp.concatenate([v_before, flow_v[:, :, :-1]], axis=2)
    diverge = ((u_next - u_prev) + (v_next - v_prev) + (raised(flow_w) - lowered(flow_w))) * 0.5

    total_y = rows_y * count_y
    n_q = 256
    n_p = total_y // n_q
    split_y = rows_y // n_q
    piece_x = rows_x // count_y
    sent = diverge.reshape(levels, count_y, piece_x, split_y, n_q).transpose(1, 3, 0, 2, 4)
    sent = sent.reshape(count_y, split_y * levels * piece_x, n_q)
    columns = lax.all_to_all(sent, "gy", split_axis=0, concat_axis=0, tiled=True)
    columns = columns.reshape(n_p, levels, piece_x, n_q)
    w1, t1c, t1s, w2 = y_tables(n_p, n_q)
    stage1 = lax.dot_general(
        const(w1), columns, (((1,), (0,)), ((), ())), precision=PREC
    )
    real1 = stage1[:n_p]
    imag1 = stage1[n_p:]
    tc = const(t1c)[:, None, None, :]
    ts = const(t1s)[:, None, None, :]
    real_t = real1 * tc + imag1 * ts
    imag_t = imag1 * tc - real1 * ts
    rows_m = levels * n_p * piece_x
    joined = jnp.concatenate(
        [real_t.reshape(rows_m, n_q), imag_t.reshape(rows_m, n_q)], axis=1
    )
    devices = count_x * count_y
    spectrum_y = lax.dot_general(
        const(w2.reshape(devices, 2, 2 * n_q)), joined, (((2,), (1,)), ((), ())), precision=PREC
    )
    moved = lax.all_to_all(spectrum_y, ("gx", "gy"), split_axis=0, concat_axis=0, tiled=True)

    total_x = rows_x * count_x
    n_s = devices
    n_i = piece_x
    scale = 1.0 / math.sqrt(total_x * total_y)
    wa, t2c, t2s, wb = x_tables(n_s, n_i, scale)
    stage_a = lax.dot_general(
        moved.reshape(2 * n_s, rows_m), const(wa), (((0,), (0,)), ((), ())), precision=PREC
    )
    batch = levels * n_p
    stage_a = stage_a.reshape(batch, n_i, 2 * n_s)
    real_a = stage_a[:, :, :n_s]
    imag_a = stage_a[:, :, n_s:]
    uc = const(t2c)[None]
    us = const(t2s)[None]
    real_b = real_a * uc + imag_a * us
    imag_b = imag_a * uc - real_a * us
    joined_x = jnp.concatenate([real_b, imag_b], axis=1)
    wbb = jnp.broadcast_to(const(wb)[None], (batch,) + wb.shape)
    result = lax.dot_general(
        wbb, joined_x, (((2,), (1,)), ((0,), (0,))), precision=PREC
    )
    result = result.reshape(n_p, levels, 2, n_i, n_s).transpose(2, 1, 0, 3, 4)
    spectrum = result.reshape(2, levels, n_p, total_x)
    return (tendency, spectrum)


def solution(mesh):
    return jax.shard_map(
        body,
        mesh=mesh,
        in_specs=(P(None, None, "gx", "gy"), P("gx", "gy"), P("gx", "gy")),
        out_specs=(P(None, None, "gx", "gy"), P(None, None, ("gx", "gy"), None)),
        check_vma=False,
    )
```

```python
import math

import numpy as np
import jax
import jax.numpy as jnp
from jax import lax
from jax.sharding import PartitionSpec as P

NU = 0.1
BETA = 0.5
HEAT = 1.0
DT = 0.5
PREC = lax.Precision.HIGH


def ring(count):
    up = [(i, (i + 1) % count) for i in range(count)]
    down = [(j, i) for i, j in up]
    return up, down


def raised(field):
    zero = jnp.zeros_like(field[:1])
    return jnp.concatenate([field[1:], zero], axis=0)


def lowered(field):
    zero = jnp.zeros_like(field[:1])
    return jnp.concatenate([zero, field[:-1]], axis=0)


def tendency_one(component, field, pick, center, fluid, surface):
    slope_x = (
        45.0 * (pick(1, 0) - pick(-1, 0))
        - 9.0 * (pick(2, 0) - pick(-2, 0))
        + (pick(3, 0) - pick(-3, 0))
    ) / 60.0
    slope_y = (
        45.0 * (pick(0, 1) - pick(0, -1))
        - 9.0 * (pick(0, 2) - pick(0, -2))
        + (pick(0, 3) - pick(0, -3))
    ) / 60.0
    above = raised(field)
    below = lowered(field)
    slope_z = (above - below) * 0.5
    advect = center[0] * slope_x + center[1] * slope_y + center[2] * slope_z
    spread = (
        pick(1, 0)
        + pick(-1, 0)
        + pick(0, 1)
        + pick(0, -1)
        - 4.0 * field
        + (above + below - 2.0 * field)
    )
    result = NU * spread - advect
    if component == 2:
        result = result + BETA * center[3]
    if component == 3:
        result = result + HEAT * surface
    return fluid * result


def cos_sin(rows, cols, length, scale=1.0):
    product = (np.arange(rows)[:, None] * np.arange(cols)[None, :]) % length
    angle = product * (2.0 * math.pi / length)
    return np.cos(angle) * scale, np.sin(angle) * scale


def const(array):
    return jnp.asarray(np.asarray(array, dtype=np.float32))


def y_tables(n_p, n_q):
    c1, s1 = cos_sin(n_p, n_p, n_p)
    w1 = np.concatenate([c1, -s1], axis=0)
    t_c, t_s = cos_sin(n_p, n_q, n_p * n_q)
    c2, s2 = cos_sin(n_q, n_q, n_q)
    w2 = np.zeros((n_q, 2, 2, n_q))
    w2[:, 0, 0] = c2
    w2[:, 0, 1] = s2
    w2[:, 1, 0] = -s2
    w2[:, 1, 1] = c2
    return w1, t_c, t_s, w2.reshape(2 * n_q, 2 * n_q)


def x_tables(n_s, n_i, scale):
    c2, s2 = cos_sin(n_s, n_s, n_s)
    wa = np.zeros((n_s, 2, 2, n_s))
    wa[:, 0, 0] = c2
    wa[:, 1, 0] = s2
    wa[:, 0, 1] = -s2
    wa[:, 1, 1] = c2
    t_c, t_s = cos_sin(n_i, n_s, n_s * n_i)
    cb, sb = cos_sin(n_i, n_i, n_i, scale)
    wb = np.zeros((2, n_i, 2, n_i))
    wb[0, :, 0] = cb
    wb[0, :, 1] = sb
    wb[1, :, 0] = -sb
    wb[1, :, 1] = cb
    return wa.reshape(2 * n_s, 2 * n_s), t_c, t_s, wb.reshape(2 * n_i, 2 * n_i)


def body(state, heights, surface_flag):
    levels = state.shape[1]
    rows_x = state.shape[2]
    rows_y = state.shape[3]
    count_x = lax.axis_size("gx")
    count_y = lax.axis_size("gy")
    up_x, down_x = ring(count_x)
    up_y, down_y = ring(count_y)

    level = lax.broadcasted_iota(jnp.int32, state.shape[1:], 0)
    fluid = (level >= heights[None]).astype(jnp.float32)
    surface = (level == heights[None]).astype(jnp.float32) * surface_flag[None].astype(jnp.float32)
    masked = state * fluid.astype(jnp.bfloat16)[None]

    x_before = lax.ppermute(masked[:, :, rows_x - 3 :, :], "gx", up_x)
    x_after = lax.ppermute(masked[:, :, :3, :], "gx", down_x)
    y_before = lax.ppermute(masked[:, :, :, rows_y - 3 :], "gy", up_y)
    y_after = lax.ppermute(masked[:, :, :, :3], "gy", down_y)
    pad_x = jnp.concatenate([x_before, masked, x_after], axis=2).astype(jnp.float32)
    pad_y = jnp.concatenate([y_before, masked, y_after], axis=3).astype(jnp.float32)
    center = masked.astype(jnp.float32)

    pieces = []
    rounded = []
    for component in range(4):

        def pick(step_x, step_y, component=component):
            if step_y == 0:
                return pad_x[component, :, 3 + step_x : 3 + step_x + rows_x, :]
            return pad_y[component, :, :, 3 + step_y : 3 + step_y + rows_y]

        exact = tendency_one(component, center[component], pick, center, fluid, surface)
        pieces.append(exact.astype(jnp.bfloat16))
        rounded.append(lax.reduce_precision(exact, exponent_bits=8, mantissa_bits=7))
    tendency = jnp.stack(pieces)

    flow_u = center[0] + DT * rounded[0]
    flow_v = center[1] + DT * rounded[1]
    flow_w = center[2] + DT * rounded[2]
    u_before = lax.ppermute(flow_u[:, rows_x - 1 :, :], "gx", up_x)
    u_after = lax.ppermute(flow_u[:, :1, :], "gx", down_x)
    u_next = jnp.concatenate([flow_u[:, 1:, :], u_after], axis=1)
    u_prev = jnp.concatenate([u_before, flow_u[:, :-1, :]], axis=1)
    zero_col = jnp.zeros_like(flow_v[:, :, :1])
    v_next = jnp.concatenate([flow_v[:, :, 1:], zero_col], axis=2)
    v_prev = jnp.concatenate([zero_col, flow_v[:, :, :-1]], axis=2)
    diverge = ((u_next - u_prev) + (v_next - v_prev) + (raised(flow_w) - lowered(flow_w))) * 0.5

    total_y = rows_y * count_y
    n_q = 256
    n_p = total_y // n_q
    split_y = rows_y // n_q
    piece_x = rows_x // count_y
    sent = diverge.reshape(levels, count_y, piece_x, split_y, n_q).transpose(1, 3, 0, 2, 4)
    main_rows = split_y * levels * piece_x
    sent = sent.reshape(count_y, main_rows, n_q)
    edges = jnp.stack([flow_v[:, :, 0], flow_v[:, :, rows_y - 1]], axis=0)
    edges = edges.reshape(2, levels, count_y, piece_x).transpose(2, 0, 1, 3)
    edge_width = 2 * levels * piece_x
    edges = edges.reshape(count_y, 1, edge_width)
    edges = jnp.pad(edges, ((0, 0), (0, 7), (0, n_q - edge_width)))
    sent = jnp.concatenate([sent, edges], axis=1)
    columns = lax.all_to_all(sent, "gy", split_axis=0, concat_axis=0, tiled=True)
    edges = columns[:, main_rows, :edge_width].reshape(count_y, 2, levels, piece_x)
    last_prev = jnp.roll(edges[:, 1], 1, axis=0)
    first_next = jnp.roll(edges[:, 0], -1, axis=0)
    columns = columns[:, :main_rows].reshape(count_y, split_y, levels, piece_x, n_q)
    q_at = lax.broadcasted_iota(jnp.int32, columns.shape, 4)
    half_at = lax.broadcasted_iota(jnp.int32, columns.shape, 1)
    columns = (
        columns
        + jnp.where((q_at == 0) & (half_at == 0), (-0.5 * last_prev)[:, None, :, :, None], 0.0)
        + jnp.where(
            (q_at == n_q - 1) & (half_at == split_y - 1), (0.5 * first_next)[:, None, :, :, None], 0.0
        )
    )
    columns = columns.reshape(n_p, levels, piece_x, n_q)
    w1, t1c, t1s, w2 = y_tables(n_p, n_q)
    stage1 = lax.dot_general(
        const(w1), columns, (((1,), (0,)), ((), ())), precision=PREC
    )
    real1 = stage1[:n_p]
    imag1 = stage1[n_p:]
    tc = const(t1c)[:, None, None, :]
    ts = const(t1s)[:, None, None, :]
    real_t = real1 * tc + imag1 * ts
    imag_t = imag1 * tc - real1 * ts
    rows_m = levels * n_p * piece_x
    joined = jnp.concatenate(
        [real_t.reshape(rows_m, n_q), imag_t.reshape(rows_m, n_q)], axis=1
    )
    devices = count_x * count_y
    spectrum_y = lax.dot_general(
        const(w2.reshape(devices, 2, 2 * n_q)), joined, (((2,), (1,)), ((), ())), precision=PREC
    )
    moved = lax.all_to_all(spectrum_y, ("gx", "gy"), split_axis=0, concat_axis=0, tiled=True)

    total_x = rows_x * count_x
    n_s = devices
    n_i = piece_x
    scale = 1.0 / math.sqrt(total_x * total_y)
    wa, t2c, t2s, wb = x_tables(n_s, n_i, scale)
    stage_a = lax.dot_general(
        moved.reshape(2 * n_s, rows_m), const(wa), (((0,), (0,)), ((), ())), precision=PREC
    )
    batch = levels * n_p
    stage_a = stage_a.reshape(batch, n_i, 2 * n_s)
    real_a = stage_a[:, :, :n_s]
    imag_a = stage_a[:, :, n_s:]
    uc = const(t2c)[None]
    us = const(t2s)[None]
    real_b = real_a * uc + imag_a * us
    imag_b = imag_a * uc - real_a * us
    joined_x = jnp.concatenate([real_b, imag_b], axis=1)
    wbb = jnp.broadcast_to(const(wb)[None], (batch,) + wb.shape)
    result = lax.dot_general(
        wbb, joined_x, (((2,), (1,)), ((0,), (0,))), precision=PREC
    )
    result = result.reshape(n_p, levels, 2, n_i, n_s).transpose(2, 1, 0, 3, 4)
    spectrum = result.reshape(2, levels, n_p, total_x)
    return (tendency, spectrum)


def solution(mesh):
    return jax.shard_map(
        body,
        mesh=mesh,
        in_specs=(P(None, None, "gx", "gy"), P("gx", "gy"), P("gx", "gy")),
        out_specs=(P(None, None, "gx", "gy"), P(None, None, ("gx", "gy"), None)),
        check_vma=False,
    )
```

```python
import math

import numpy as np
import jax
import jax.numpy as jnp
from jax import lax
from jax.sharding import PartitionSpec as P


NU = 0.1
BETA = 0.5
HEAT = 1.0
DT = 0.5
PREC = lax.Precision.HIGH


def ring(count):
    up = [(i, (i + 1) % count) for i in range(count)]
    down = [(j, i) for i, j in up]
    return up, down


def raised(field):
    zero = jnp.zeros_like(field[:1])
    return jnp.concatenate([field[1:], zero], axis=0)


def lowered(field):
    zero = jnp.zeros_like(field[:1])
    return jnp.concatenate([zero, field[:-1]], axis=0)


def tendency_one(component, field, pick, center, fluid, surface):
    slope_x = (
        45.0 * (pick(1, 0) - pick(-1, 0))
        - 9.0 * (pick(2, 0) - pick(-2, 0))
        + (pick(3, 0) - pick(-3, 0))
    ) / 60.0
    slope_y = (
        45.0 * (pick(0, 1) - pick(0, -1))
        - 9.0 * (pick(0, 2) - pick(0, -2))
        + (pick(0, 3) - pick(0, -3))
    ) / 60.0
    above = raised(field)
    below = lowered(field)
    slope_z = (above - below) * 0.5
    advect = center[0] * slope_x + center[1] * slope_y + center[2] * slope_z
    spread = (
        pick(1, 0)
        + pick(-1, 0)
        + pick(0, 1)
        + pick(0, -1)
        - 4.0 * field
        + (above + below - 2.0 * field)
    )
    result = NU * spread - advect
    if component == 2:
        result = result + BETA * center[3]
    if component == 3:
        result = result + HEAT * surface
    return fluid * result


def cos_sin(rows, cols, length, scale=1.0):
    product = (np.arange(rows)[:, None] * np.arange(cols)[None, :]) % length
    angle = product * (2.0 * math.pi / length)
    return np.cos(angle) * scale, np.sin(angle) * scale


def const(array):
    return jnp.asarray(np.asarray(array, dtype=np.float32))


def y_tables(n_p, n_q):
    c1, s1 = cos_sin(n_p, n_p, n_p)
    w1 = np.concatenate([c1, -s1], axis=0)
    t_c, t_s = cos_sin(n_p, n_q, n_p * n_q)
    c2, s2 = cos_sin(n_q, n_q, n_q)
    w2 = np.zeros((n_q, 2, 2, n_q))
    w2[:, 0, 0] = c2
    w2[:, 0, 1] = s2
    w2[:, 1, 0] = -s2
    w2[:, 1, 1] = c2
    return w1, t_c, t_s, w2.reshape(2 * n_q, 2 * n_q)


def x_tables(n_s, n_i, scale):
    c2, s2 = cos_sin(n_s, n_s, n_s)
    wa = np.zeros((n_s, 2, 2, n_s))
    wa[:, 0, 0] = c2
    wa[:, 1, 0] = s2
    wa[:, 0, 1] = -s2
    wa[:, 1, 1] = c2
    t_c, t_s = cos_sin(n_i, n_s, n_s * n_i)
    cb, sb = cos_sin(n_i, n_i, n_i, scale)
    wb = np.zeros((2, n_i, 2, n_i))
    wb[0, :, 0] = cb
    wb[0, :, 1] = sb
    wb[1, :, 0] = -sb
    wb[1, :, 1] = cb
    return wa.reshape(2 * n_s, 2 * n_s), t_c, t_s, wb.reshape(2 * n_i, 2 * n_i)


def body(state, heights, surface_flag):
    levels = state.shape[1]
    rows_x = state.shape[2]
    rows_y = state.shape[3]
    count_x = lax.axis_size("gx")
    count_y = lax.axis_size("gy")
    up_x, down_x = ring(count_x)
    up_y, down_y = ring(count_y)

    level = lax.broadcasted_iota(jnp.int32, state.shape[1:], 0)
    fluid = (level >= heights[None]).astype(jnp.float32)
    surface = (level == heights[None]).astype(jnp.float32) * surface_flag[None].astype(jnp.float32)
    masked = state * fluid.astype(jnp.bfloat16)[None]

    halo = 4
    held = jnp.concatenate([masked, fluid.astype(jnp.bfloat16)[None]], axis=0)
    lo_x, hi_x = slice(0, halo), slice(rows_x - halo, rows_x)
    lo_y, hi_y = slice(0, halo), slice(rows_y - halo, rows_y)
    x_before = lax.ppermute(held[:, :, hi_x, :], "gx", up_x)
    x_after = lax.ppermute(held[:, :, lo_x, :], "gx", down_x)
    y_before = lax.ppermute(held[:, :, :, hi_y], "gy", up_y)
    y_after = lax.ppermute(held[:, :, :, lo_y], "gy", down_y)

    def diagonal(step_x, step_y):
        return [
            (a * count_y + b, ((a + step_x) % count_x) * count_y + (b + step_y) % count_y)
            for a in range(count_x)
            for b in range(count_y)
        ]

    both = ("gx", "gy")
    corner_mm = lax.ppermute(held[:, :, hi_x, hi_y], both, diagonal(1, 1))
    corner_mp = lax.ppermute(held[:, :, hi_x, lo_y], both, diagonal(1, -1))
    corner_pm = lax.ppermute(held[:, :, lo_x, hi_y], both, diagonal(-1, 1))
    corner_pp = lax.ppermute(held[:, :, lo_x, lo_y], both, diagonal(-1, -1))

    pad_x = jnp.concatenate(
        [x_before[:4, :, 1:], masked, x_after[:4, :, :3]], axis=2
    ).astype(jnp.float32)
    pad_y = jnp.concatenate(
        [y_before[:4, :, :, 1:], masked, y_after[:4, :, :, :3]], axis=3
    ).astype(jnp.float32)
    center = masked.astype(jnp.float32)

    pieces = []
    rounded = []
    for component in range(4):

        def pick(step_x, step_y, component=component):
            if step_y == 0:
                return pad_x[component, :, 3 + step_x : 3 + step_x + rows_x, :]
            return pad_y[component, :, :, 3 + step_y : 3 + step_y + rows_y]

        exact = tendency_one(component, center[component], pick, center, fluid, surface)
        pieces.append(exact.astype(jnp.bfloat16))
        rounded.append(lax.reduce_precision(exact, exponent_bits=8, mantissa_bits=7))

    def star_line(component, strip, line, along_x):
        strip = strip.astype(jnp.float32)
        line = line.astype(jnp.float32)
        if along_x:
            width = strip.shape[3]
            cut = lambda a, i: a[:, :, i : i + 1, :]
            ext = lambda a, i: a[:, :, :, i : i + width]
        else:
            width = strip.shape[2]
            cut = lambda a, i: a[:, :, :, i : i + 1]
            ext = lambda a, i: a[:, :, i : i + width, :]
        mid = cut(strip, 3)

        def pick(step_x, step_y):
            across, along = (step_x, step_y) if along_x else (step_y, step_x)
            if along == 0:
                return cut(strip, 3 + across)[component]
            return ext(line, halo + along)[component]

        exact = tendency_one(component, mid[component], pick, mid, mid[4], None)
        return mid[component] + DT * lax.reduce_precision(exact, exponent_bits=8, mantissa_bits=7)

    top = jnp.concatenate([x_before, held[:, :, :3]], axis=2)
    top_line = jnp.concatenate([corner_mm, x_before, corner_mp], axis=3)[:, :, halo - 1 : halo]
    bottom = jnp.concatenate([held[:, :, rows_x - 3 :], x_after], axis=2)
    bottom_line = jnp.concatenate([corner_pm, x_after, corner_pp], axis=3)[:, :, :1]
    left = jnp.concatenate([y_before, held[:, :, :, :3]], axis=3)
    left_line = jnp.concatenate([corner_mm, y_before, corner_pm], axis=2)[:, :, :, halo - 1 : halo]
    right = jnp.concatenate([held[:, :, :, rows_y - 3 :], y_after], axis=3)
    right_line = jnp.concatenate([corner_mp, y_after, corner_pp], axis=2)[:, :, :, :1]
    u_before = star_line(0, top, top_line, True)
    u_after = star_line(0, bottom, bottom_line, True)
    v_before = star_line(1, left, left_line, False)
    v_after = star_line(1, right, right_line, False)
    tendency = jnp.stack(pieces)

    flow_u = center[0] + DT * rounded[0]
    flow_v = center[1] + DT * rounded[1]
    flow_w = center[2] + DT * rounded[2]
    u_next = jnp.concatenate([flow_u[:, 1:, :], u_after], axis=1)
    u_prev = jnp.concatenate([u_before, flow_u[:, :-1, :]], axis=1)
    v_next = jnp.concatenate([flow_v[:, :, 1:], v_after], axis=2)
    v_prev = jnp.concatenate([v_before, flow_v[:, :, :-1]], axis=2)
    diverge = ((u_next - u_prev) + (v_next - v_prev) + (raised(flow_w) - lowered(flow_w))) * 0.5

    total_y = rows_y * count_y
    n_q = 256
    n_p = total_y // n_q
    split_y = rows_y // n_q
    piece_x = rows_x // count_y
    sent = diverge.reshape(levels, count_y, piece_x, split_y, n_q).transpose(1, 3, 0, 2, 4)
    sent = sent.reshape(count_y, split_y * levels * piece_x, n_q)
    columns = lax.all_to_all(sent, "gy", split_axis=0, concat_axis=0, tiled=True)
    columns = columns.reshape(n_p, levels, piece_x, n_q)
    w1, t1c, t1s, w2 = y_tables(n_p, n_q)
    stage1 = lax.dot_general(
        const(w1), columns, (((1,), (0,)), ((), ())), precision=PREC
    )
    real1 = stage1[:n_p]
    imag1 = stage1[n_p:]
    tc = const(t1c)[:, None, None, :]
    ts = const(t1s)[:, None, None, :]
    real_t = real1 * tc + imag1 * ts
    imag_t = imag1 * tc - real1 * ts
    rows_m = levels * n_p * piece_x
    joined = jnp.concatenate(
        [real_t.reshape(rows_m, n_q), imag_t.reshape(rows_m, n_q)], axis=1
    )
    devices = count_x * count_y
    spectrum_y = lax.dot_general(
        const(w2.reshape(devices, 2, 2 * n_q)), joined, (((2,), (1,)), ((), ())), precision=PREC
    )
    moved = lax.all_to_all(spectrum_y, ("gx", "gy"), split_axis=0, concat_axis=0, tiled=True)

    total_x = rows_x * count_x
    n_s = devices
    n_i = piece_x
    scale = 1.0 / math.sqrt(total_x * total_y)
    wa, t2c, t2s, wb = x_tables(n_s, n_i, scale)
    stage_a = lax.dot_general(
        moved.reshape(2 * n_s, rows_m), const(wa), (((0,), (0,)), ((), ())), precision=PREC
    )
    batch = levels * n_p
    stage_a = stage_a.reshape(batch, n_i, 2 * n_s)
    real_a = stage_a[:, :, :n_s]
    imag_a = stage_a[:, :, n_s:]
    uc = const(t2c)[None]
    us = const(t2s)[None]
    real_b = real_a * uc + imag_a * us
    imag_b = imag_a * uc - real_a * us
    joined_x = jnp.concatenate([real_b, imag_b], axis=1)
    wbb = jnp.broadcast_to(const(wb)[None], (batch,) + wb.shape)
    result = lax.dot_general(
        wbb, joined_x, (((2,), (1,)), ((0,), (0,))), precision=PREC
    )
    result = result.reshape(n_p, levels, 2, n_i, n_s).transpose(2, 1, 0, 3, 4)
    spectrum = result.reshape(2, levels, n_p, total_x)
    return (tendency, spectrum)


def solution(mesh):
    return jax.shard_map(
        body,
        mesh=mesh,
        in_specs=(P(None, None, "gx", "gy"), P("gx", "gy"), P("gx", "gy")),
        out_specs=(P(None, None, "gx", "gy"), P(None, None, ("gx", "gy"), None)),
        check_vma=False,
    )
```

```python
import math

import numpy as np
import jax
import jax.numpy as jnp
from jax import lax
from jax.sharding import PartitionSpec as P


NU = 0.1
BETA = 0.5
HEAT = 1.0
DT = 0.5
PREC = lax.Precision.HIGH


def ring(count):
    up = [(i, (i + 1) % count) for i in range(count)]
    down = [(j, i) for i, j in up]
    return up, down


def raised(field):
    zero = jnp.zeros_like(field[:1])
    return jnp.concatenate([field[1:], zero], axis=0)


def lowered(field):
    zero = jnp.zeros_like(field[:1])
    return jnp.concatenate([zero, field[:-1]], axis=0)


def tendency_one(component, field, pick, center, fluid, surface):
    slope_x = (
        45.0 * (pick(1, 0) - pick(-1, 0))
        - 9.0 * (pick(2, 0) - pick(-2, 0))
        + (pick(3, 0) - pick(-3, 0))
    ) / 60.0
    slope_y = (
        45.0 * (pick(0, 1) - pick(0, -1))
        - 9.0 * (pick(0, 2) - pick(0, -2))
        + (pick(0, 3) - pick(0, -3))
    ) / 60.0
    above = raised(field)
    below = lowered(field)
    slope_z = (above - below) * 0.5
    advect = center[0] * slope_x + center[1] * slope_y + center[2] * slope_z
    spread = (
        pick(1, 0)
        + pick(-1, 0)
        + pick(0, 1)
        + pick(0, -1)
        - 4.0 * field
        + (above + below - 2.0 * field)
    )
    result = NU * spread - advect
    if component == 2:
        result = result + BETA * center[3]
    if component == 3:
        result = result + HEAT * surface
    return fluid * result


def cos_sin(rows, cols, length, scale=1.0):
    product = (np.arange(rows)[:, None] * np.arange(cols)[None, :]) % length
    angle = product * (2.0 * math.pi / length)
    return np.cos(angle) * scale, np.sin(angle) * scale


def const(array):
    return jnp.asarray(np.asarray(array, dtype=np.float32))


def y_tables(n_p, n_q):
    c1, s1 = cos_sin(n_p, n_p, n_p)
    w1 = np.concatenate([c1, -s1], axis=0)
    t_c, t_s = cos_sin(n_p, n_q, n_p * n_q)
    c2, s2 = cos_sin(n_q, n_q, n_q)
    w2 = np.zeros((n_q, 2, 2, n_q))
    w2[:, 0, 0] = c2
    w2[:, 0, 1] = s2
    w2[:, 1, 0] = -s2
    w2[:, 1, 1] = c2
    return w1, t_c, t_s, w2.reshape(2 * n_q, 2 * n_q)


def x_tables(n_s, n_i, scale):
    c2, s2 = cos_sin(n_s, n_s, n_s)
    wa = np.zeros((n_s, 2, 2, n_s))
    wa[:, 0, 0] = c2
    wa[:, 1, 0] = s2
    wa[:, 0, 1] = -s2
    wa[:, 1, 1] = c2
    t_c, t_s = cos_sin(n_i, n_s, n_s * n_i)
    cb, sb = cos_sin(n_i, n_i, n_i, scale)
    wb = np.zeros((2, n_i, 2, n_i))
    wb[0, :, 0] = cb
    wb[0, :, 1] = sb
    wb[1, :, 0] = -sb
    wb[1, :, 1] = cb
    return wa.reshape(2 * n_s, 2 * n_s), t_c, t_s, wb.reshape(2 * n_i, 2 * n_i)


def body(state, heights, surface_flag):
    levels = state.shape[1]
    rows_x = state.shape[2]
    rows_y = state.shape[3]
    count_x = lax.axis_size("gx")
    count_y = lax.axis_size("gy")
    up_x, down_x = ring(count_x)
    up_y, down_y = ring(count_y)

    level = lax.broadcasted_iota(jnp.int32, state.shape[1:], 0)
    fluid = (level >= heights[None]).astype(jnp.float32)
    surface = (level == heights[None]).astype(jnp.float32) * surface_flag[None].astype(jnp.float32)
    masked = state * fluid.astype(jnp.bfloat16)[None]

    def masked_part(xs, ys):
        lev = lax.broadcasted_iota(jnp.int32, (levels, xs.stop - xs.start, ys.stop - ys.start), 0)
        wet = (lev >= heights[None, xs, ys]).astype(jnp.bfloat16)
        return state[:, :, xs, ys] * wet[None]

    all_x, all_y = slice(0, rows_x), slice(0, rows_y)
    x_before = lax.ppermute(masked_part(slice(rows_x - 3, rows_x), all_y), "gx", up_x)
    x_after = lax.ppermute(masked_part(slice(0, 3), all_y), "gx", down_x)

    def lanes_x(part):
        return jnp.swapaxes(part, 2, 3).reshape(-1, rows_x)

    def from_lanes_x(flat):
        return jnp.swapaxes(flat.reshape(state.shape[0], levels, 3, rows_x), 2, 3)

    y_before = from_lanes_x(
        lax.ppermute(lanes_x(masked_part(all_x, slice(rows_y - 3, rows_y))), "gy", up_y)
    )
    y_after = from_lanes_x(lax.ppermute(lanes_x(masked_part(all_x, slice(0, 3))), "gy", down_y))
    pad_x = jnp.concatenate([x_before, masked, x_after], axis=2).astype(jnp.float32)
    pad_y = jnp.concatenate([y_before, masked, y_after], axis=3).astype(jnp.float32)
    center = masked.astype(jnp.float32)

    pieces = []
    rounded = []
    for component in range(4):

        def pick(step_x, step_y, component=component):
            if step_y == 0:
                return pad_x[component, :, 3 + step_x : 3 + step_x + rows_x, :]
            return pad_y[component, :, :, 3 + step_y : 3 + step_y + rows_y]

        exact = tendency_one(component, center[component], pick, center, fluid, surface)
        pieces.append(exact.astype(jnp.bfloat16))
        rounded.append(lax.reduce_precision(exact, exponent_bits=8, mantissa_bits=7))
    tendency = jnp.stack(pieces)

    flows = []
    for component in range(3):
        flows.append(center[component] + DT * rounded[component])
    flow_u, flow_v, flow_w = flows
    u_before = lax.ppermute(flow_u[:, rows_x - 1 :, :], "gx", up_x)
    u_after = lax.ppermute(flow_u[:, :1, :], "gx", down_x)
    v_before = jnp.swapaxes(
        lax.ppermute(jnp.swapaxes(flow_v[:, :, rows_y - 1 :], 1, 2), "gy", up_y), 1, 2
    )
    v_after = jnp.swapaxes(lax.ppermute(jnp.swapaxes(flow_v[:, :, :1], 1, 2), "gy", down_y), 1, 2)
    u_next = jnp.concatenate([flow_u[:, 1:, :], u_after], axis=1)
    u_prev = jnp.concatenate([u_before, flow_u[:, :-1, :]], axis=1)
    v_next = jnp.concatenate([flow_v[:, :, 1:], v_after], axis=2)
    v_prev = jnp.concatenate([v_before, flow_v[:, :, :-1]], axis=2)
    diverge = ((u_next - u_prev) + (v_next - v_prev) + (raised(flow_w) - lowered(flow_w))) * 0.5

    total_y = rows_y * count_y
    n_q = 256
    n_p = total_y // n_q
    split_y = rows_y // n_q
    piece_x = rows_x // count_y
    sent = diverge.reshape(levels, count_y, piece_x, split_y, n_q).transpose(1, 3, 0, 2, 4)
    sent = sent.reshape(count_y, split_y * levels * piece_x, n_q)
    columns = lax.all_to_all(sent, "gy", split_axis=0, concat_axis=0, tiled=True)
    columns = columns.reshape(n_p, levels, piece_x, n_q)
    w1, t1c, t1s, w2 = y_tables(n_p, n_q)
    stage1 = lax.dot_general(
        const(w1), columns, (((1,), (0,)), ((), ())), precision=PREC
    )
    real1 = stage1[:n_p]
    imag1 = stage1[n_p:]
    tc = const(t1c)[:, None, None, :]
    ts = const(t1s)[:, None, None, :]
    real_t = real1 * tc + imag1 * ts
    imag_t = imag1 * tc - real1 * ts
    rows_m = levels * n_p * piece_x
    joined = jnp.concatenate(
        [real_t.reshape(rows_m, n_q), imag_t.reshape(rows_m, n_q)], axis=1
    )
    devices = count_x * count_y
    spectrum_y = lax.dot_general(
        const(w2.reshape(devices, 2, 2 * n_q)), joined, (((2,), (1,)), ((), ())), precision=PREC
    )
    moved = lax.all_to_all(spectrum_y, ("gx", "gy"), split_axis=0, concat_axis=0, tiled=True)

    total_x = rows_x * count_x
    n_s = devices
    n_i = piece_x
    scale = 1.0 / math.sqrt(total_x * total_y)
    wa, t2c, t2s, wb = x_tables(n_s, n_i, scale)
    stage_a = lax.dot_general(
        moved.reshape(2 * n_s, rows_m), const(wa), (((0,), (0,)), ((), ())), precision=PREC
    )
    batch = levels * n_p
    stage_a = stage_a.reshape(batch, n_i, 2 * n_s)
    real_a = stage_a[:, :, :n_s]
    imag_a = stage_a[:, :, n_s:]
    uc = const(t2c)[None]
    us = const(t2s)[None]
    real_b = real_a * uc + imag_a * us
    imag_b = imag_a * uc - real_a * us
    joined_x = jnp.concatenate([real_b, imag_b], axis=1)
    wbb = jnp.broadcast_to(const(wb)[None], (batch,) + wb.shape)
    result = lax.dot_general(
        wbb, joined_x, (((2,), (1,)), ((0,), (0,))), precision=PREC
    )
    result = result.reshape(n_p, levels, 2, n_i, n_s).transpose(2, 1, 0, 3, 4)
    spectrum = result.reshape(2, levels, n_p, total_x)
    return (tendency, spectrum)


def solution(mesh):
    return jax.shard_map(
        body,
        mesh=mesh,
        in_specs=(P(None, None, "gx", "gy"), P("gx", "gy"), P("gx", "gy")),
        out_specs=(P(None, None, "gx", "gy"), P(None, None, ("gx", "gy"), None)),
        check_vma=False,
    )
```

```python
import math

import numpy as np
import jax
import jax.numpy as jnp
from jax import lax
from jax.sharding import PartitionSpec as P


NU = 0.1
BETA = 0.5
HEAT = 1.0
DT = 0.5
PREC = lax.Precision.HIGH


def ring(count):
    up = [(i, (i + 1) % count) for i in range(count)]
    down = [(j, i) for i, j in up]
    return up, down


def raised(field):
    zero = jnp.zeros_like(field[:1])
    return jnp.concatenate([field[1:], zero], axis=0)


def lowered(field):
    zero = jnp.zeros_like(field[:1])
    return jnp.concatenate([zero, field[:-1]], axis=0)


def tendency_one(component, field, pick, center, fluid, surface):
    slope_x = (
        45.0 * (pick(1, 0) - pick(-1, 0))
        - 9.0 * (pick(2, 0) - pick(-2, 0))
        + (pick(3, 0) - pick(-3, 0))
    ) / 60.0
    slope_y = (
        45.0 * (pick(0, 1) - pick(0, -1))
        - 9.0 * (pick(0, 2) - pick(0, -2))
        + (pick(0, 3) - pick(0, -3))
    ) / 60.0
    above = raised(field)
    below = lowered(field)
    slope_z = (above - below) * 0.5
    advect = center[0] * slope_x + center[1] * slope_y + center[2] * slope_z
    spread = (
        pick(1, 0)
        + pick(-1, 0)
        + pick(0, 1)
        + pick(0, -1)
        - 4.0 * field
        + (above + below - 2.0 * field)
    )
    result = NU * spread - advect
    if component == 2:
        result = result + BETA * center[3]
    if component == 3:
        result = result + HEAT * surface
    return fluid * result


def cos_sin(rows, cols, length, scale=1.0):
    product = (np.arange(rows)[:, None] * np.arange(cols)[None, :]) % length
    angle = product * (2.0 * math.pi / length)
    return np.cos(angle) * scale, np.sin(angle) * scale


def const(array):
    return jnp.asarray(np.asarray(array, dtype=np.float32))


def y_tables(n_p, n_q):
    c1, s1 = cos_sin(n_p, n_p, n_p)
    w1 = np.concatenate([c1, -s1], axis=0)
    t_c, t_s = cos_sin(n_p, n_q, n_p * n_q)
    c2, s2 = cos_sin(n_q, n_q, n_q)
    w2 = np.zeros((n_q, 2, 2, n_q))
    w2[:, 0, 0] = c2
    w2[:, 0, 1] = s2
    w2[:, 1, 0] = -s2
    w2[:, 1, 1] = c2
    return w1, t_c, t_s, w2.reshape(2 * n_q, 2 * n_q)


def x_tables(n_s, n_i, scale):
    c2, s2 = cos_sin(n_s, n_s, n_s)
    wa = np.zeros((n_s, 2, 2, n_s))
    wa[:, 0, 0] = c2
    wa[:, 1, 0] = s2
    wa[:, 0, 1] = -s2
    wa[:, 1, 1] = c2
    t_c, t_s = cos_sin(n_i, n_s, n_s * n_i)
    cb, sb = cos_sin(n_i, n_i, n_i, scale)
    wb = np.zeros((2, n_i, 2, n_i))
    wb[0, :, 0] = cb
    wb[0, :, 1] = sb
    wb[1, :, 0] = -sb
    wb[1, :, 1] = cb
    return wa.reshape(2 * n_s, 2 * n_s), t_c, t_s, wb.reshape(2 * n_i, 2 * n_i)


def body(state, heights, surface_flag):
    levels = state.shape[1]
    rows_x = state.shape[2]
    rows_y = state.shape[3]
    count_x = lax.axis_size("gx")
    count_y = lax.axis_size("gy")
    up_x, down_x = ring(count_x)
    up_y, down_y = ring(count_y)

    level = lax.broadcasted_iota(jnp.int32, state.shape[1:], 0)
    fluid = (level >= heights[None]).astype(jnp.float32)
    surface = (level == heights[None]).astype(jnp.float32) * surface_flag[None].astype(jnp.float32)
    masked = state * fluid.astype(jnp.bfloat16)[None]

    def masked_part(xs, ys):
        lev = lax.broadcasted_iota(jnp.int32, (levels, xs.stop - xs.start, ys.stop - ys.start), 0)
        wet = (lev >= heights[None, xs, ys]).astype(jnp.bfloat16)
        return state[:, :, xs, ys] * wet[None]

    all_x, all_y = slice(0, rows_x), slice(0, rows_y)
    x_before = lax.ppermute(masked_part(slice(rows_x - 3, rows_x), all_y), "gx", up_x)
    x_after = lax.ppermute(masked_part(slice(0, 3), all_y), "gx", down_x)

    def lanes_x(part):
        return jnp.swapaxes(part, 2, 3).reshape(-1, rows_x)

    def from_lanes_x(flat):
        return jnp.swapaxes(flat.reshape(state.shape[0], levels, 3, rows_x), 2, 3)

    y_before = from_lanes_x(
        lax.ppermute(lanes_x(masked_part(all_x, slice(rows_y - 3, rows_y))), "gy", up_y)
    )
    y_after = from_lanes_x(lax.ppermute(lanes_x(masked_part(all_x, slice(0, 3))), "gy", down_y))
    pad_x = jnp.concatenate([x_before, masked, x_after], axis=2).astype(jnp.float32)
    pad_y = jnp.concatenate([y_before, masked, y_after], axis=3).astype(jnp.float32)
    center = masked.astype(jnp.float32)

    pieces = []
    rounded = []
    for component in range(4):

        def pick(step_x, step_y, component=component):
            if step_y == 0:
                return pad_x[component, :, 3 + step_x : 3 + step_x + rows_x, :]
            return pad_y[component, :, :, 3 + step_y : 3 + step_y + rows_y]

        exact = tendency_one(component, center[component], pick, center, fluid, surface)
        pieces.append(exact.astype(jnp.bfloat16))
        rounded.append(lax.reduce_precision(exact, exponent_bits=8, mantissa_bits=7))
    tendency = jnp.stack(pieces)

    flows = []
    for component in range(3):
        flows.append(center[component] + DT * rounded[component])
    flow_u, flow_v, flow_w = flows
    u_before = lax.ppermute(flow_u[:, rows_x - 1 :, :], "gx", up_x)
    u_after = lax.ppermute(flow_u[:, :1, :], "gx", down_x)
    v_before = lax.ppermute(flow_v[:, :, rows_y - 1 :], "gy", up_y)
    v_after = lax.ppermute(flow_v[:, :, :1], "gy", down_y)
    u_next = jnp.concatenate([flow_u[:, 1:, :], u_after], axis=1)
    u_prev = jnp.concatenate([u_before, flow_u[:, :-1, :]], axis=1)
    v_next = jnp.concatenate([flow_v[:, :, 1:], v_after], axis=2)
    v_prev = jnp.concatenate([v_before, flow_v[:, :, :-1]], axis=2)
    diverge = ((u_next - u_prev) + (v_next - v_prev) + (raised(flow_w) - lowered(flow_w))) * 0.5

    total_y = rows_y * count_y
    n_q = 256
    n_p = total_y // n_q
    split_y = rows_y // n_q
    piece_x = rows_x // count_y
    sent = diverge.reshape(levels, count_y, piece_x, split_y, n_q).transpose(1, 3, 0, 2, 4)
    sent = sent.reshape(count_y, split_y * levels * piece_x, n_q)
    columns = lax.all_to_all(sent, "gy", split_axis=0, concat_axis=0, tiled=True)
    columns = columns.reshape(n_p, levels, piece_x, n_q)
    w1, t1c, t1s, w2 = y_tables(n_p, n_q)
    stage1 = lax.dot_general(
        const(w1), columns, (((1,), (0,)), ((), ())), precision=PREC
    )
    real1 = stage1[:n_p]
    imag1 = stage1[n_p:]
    tc = const(t1c)[:, None, None, :]
    ts = const(t1s)[:, None, None, :]
    real_t = real1 * tc + imag1 * ts
    imag_t = imag1 * tc - real1 * ts
    rows_m = levels * n_p * piece_x
    joined = jnp.concatenate(
        [real_t.reshape(rows_m, n_q), imag_t.reshape(rows_m, n_q)], axis=1
    )
    devices = count_x * count_y
    spectrum_y = lax.dot_general(
        const(w2.reshape(devices, 2, 2 * n_q)), joined, (((2,), (1,)), ((), ())), precision=PREC
    )
    moved = lax.all_to_all(spectrum_y, ("gx", "gy"), split_axis=0, concat_axis=0, tiled=True)

    total_x = rows_x * count_x
    n_s = devices
    n_i = piece_x
    scale = 1.0 / math.sqrt(total_x * total_y)
    wa, t2c, t2s, wb = x_tables(n_s, n_i, scale)
    stage_a = lax.dot_general(
        moved.reshape(2 * n_s, rows_m), const(wa), (((0,), (0,)), ((), ())), precision=PREC
    )
    batch = levels * n_p
    stage_a = stage_a.reshape(batch, n_i, 2 * n_s)
    real_a = stage_a[:, :, :n_s]
    imag_a = stage_a[:, :, n_s:]
    uc = const(t2c)[None]
    us = const(t2s)[None]
    real_b = real_a * uc + imag_a * us
    imag_b = imag_a * uc - real_a * us
    joined_x = jnp.concatenate([real_b, imag_b], axis=1)
    wbb = jnp.broadcast_to(const(wb)[None], (batch,) + wb.shape)
    result = lax.dot_general(
        wbb, joined_x, (((2,), (1,)), ((0,), (0,))), precision=PREC
    )
    result = result.reshape(n_p, levels, 2, n_i, n_s).transpose(2, 1, 0, 3, 4)
    spectrum = result.reshape(2, levels, n_p, total_x)
    return (tendency, spectrum)


def solution(mesh):
    return jax.shard_map(
        body,
        mesh=mesh,
        in_specs=(P(None, None, "gx", "gy"), P("gx", "gy"), P("gx", "gy")),
        out_specs=(P(None, None, "gx", "gy"), P(None, None, ("gx", "gy"), None)),
        check_vma=False,
    )
```

```python
import math

import numpy as np
import jax
import jax.numpy as jnp
from jax import lax
from jax.sharding import PartitionSpec as P


NU = 0.1
BETA = 0.5
HEAT = 1.0
DT = 0.5
PREC = lax.Precision.HIGH


def ring(count):
    up = [(i, (i + 1) % count) for i in range(count)]
    down = [(j, i) for i, j in up]
    return up, down


def raised(field):
    zero = jnp.zeros_like(field[:1])
    return jnp.concatenate([field[1:], zero], axis=0)


def lowered(field):
    zero = jnp.zeros_like(field[:1])
    return jnp.concatenate([zero, field[:-1]], axis=0)


def tendency_one(component, field, pick, center, fluid, surface):
    slope_x = (
        45.0 * (pick(1, 0) - pick(-1, 0))
        - 9.0 * (pick(2, 0) - pick(-2, 0))
        + (pick(3, 0) - pick(-3, 0))
    ) / 60.0
    slope_y = (
        45.0 * (pick(0, 1) - pick(0, -1))
        - 9.0 * (pick(0, 2) - pick(0, -2))
        + (pick(0, 3) - pick(0, -3))
    ) / 60.0
    above = raised(field)
    below = lowered(field)
    slope_z = (above - below) * 0.5
    advect = center[0] * slope_x + center[1] * slope_y + center[2] * slope_z
    spread = (
        pick(1, 0)
        + pick(-1, 0)
        + pick(0, 1)
        + pick(0, -1)
        - 4.0 * field
        + (above + below - 2.0 * field)
    )
    result = NU * spread - advect
    if component == 2:
        result = result + BETA * center[3]
    if component == 3:
        result = result + HEAT * surface
    return fluid * result


def cos_sin(rows, cols, length, scale=1.0):
    product = (np.arange(rows)[:, None] * np.arange(cols)[None, :]) % length
    angle = product * (2.0 * math.pi / length)
    return np.cos(angle) * scale, np.sin(angle) * scale


def const(array):
    return jnp.asarray(np.asarray(array, dtype=np.float32))


def y_tables(n_p, n_q):
    c1, s1 = cos_sin(n_p, n_p, n_p)
    w1 = np.concatenate([c1, -s1], axis=0)
    t_c, t_s = cos_sin(n_p, n_q, n_p * n_q)
    c2, s2 = cos_sin(n_q, n_q, n_q)
    w2 = np.zeros((n_q, 2, 2, n_q))
    w2[:, 0, 0] = c2
    w2[:, 0, 1] = s2
    w2[:, 1, 0] = -s2
    w2[:, 1, 1] = c2
    return w1, t_c, t_s, w2.reshape(2 * n_q, 2 * n_q)


def x_tables(n_s, n_i, scale):
    c2, s2 = cos_sin(n_s, n_s, n_s)
    wa = np.zeros((n_s, 2, 2, n_s))
    wa[:, 0, 0] = c2
    wa[:, 1, 0] = s2
    wa[:, 0, 1] = -s2
    wa[:, 1, 1] = c2
    t_c, t_s = cos_sin(n_i, n_s, n_s * n_i)
    cb, sb = cos_sin(n_i, n_i, n_i, scale)
    wb = np.zeros((2, n_i, 2, n_i))
    wb[0, :, 0] = cb
    wb[0, :, 1] = sb
    wb[1, :, 0] = -sb
    wb[1, :, 1] = cb
    return wa.reshape(2 * n_s, 2 * n_s), t_c, t_s, wb.reshape(2 * n_i, 2 * n_i)


def body(state, heights, surface_flag):
    levels = state.shape[1]
    rows_x = state.shape[2]
    rows_y = state.shape[3]
    count_x = lax.axis_size("gx")
    count_y = lax.axis_size("gy")
    up_x, down_x = ring(count_x)
    up_y, down_y = ring(count_y)

    level = lax.broadcasted_iota(jnp.int32, state.shape[1:], 0)
    fluid = (level >= heights[None]).astype(jnp.float32)
    surface = (level == heights[None]).astype(jnp.float32) * surface_flag[None].astype(jnp.float32)
    masked = state * fluid.astype(jnp.bfloat16)[None]

    def masked_part(xs, ys):
        lev = lax.broadcasted_iota(jnp.int32, (levels, xs.stop - xs.start, ys.stop - ys.start), 0)
        wet = (lev >= heights[None, xs, ys]).astype(jnp.bfloat16)
        return state[:, :, xs, ys] * wet[None]

    all_x, all_y = slice(0, rows_x), slice(0, rows_y)
    x_before = lax.ppermute(masked_part(slice(rows_x - 3, rows_x), all_y), "gx", up_x)
    x_after = lax.ppermute(masked_part(slice(0, 3), all_y), "gx", down_x)
    y_before = lax.ppermute(masked_part(all_x, slice(rows_y - 3, rows_y)), "gy", up_y)
    y_after = lax.ppermute(masked_part(all_x, slice(0, 3)), "gy", down_y)
    pad_x = jnp.concatenate([x_before, masked, x_after], axis=2).astype(jnp.float32)
    pad_y = jnp.concatenate([y_before, masked, y_after], axis=3).astype(jnp.float32)
    center = masked.astype(jnp.float32)

    pieces = []
    rounded = []
    for component in range(4):

        def pick(step_x, step_y, component=component):
            if step_y == 0:
                return pad_x[component, :, 3 + step_x : 3 + step_x + rows_x, :]
            return pad_y[component, :, :, 3 + step_y : 3 + step_y + rows_y]

        exact = tendency_one(component, center[component], pick, center, fluid, surface)
        pieces.append(exact.astype(jnp.bfloat16))
        rounded.append(lax.reduce_precision(exact, exponent_bits=8, mantissa_bits=7))
    tendency = jnp.stack(pieces)

    flows = []
    for component in range(3):
        flows.append(center[component] + DT * rounded[component])
    flow_u, flow_v, flow_w = flows
    u_before = lax.ppermute(flow_u[:, rows_x - 1 :, :], "gx", up_x)
    u_after = lax.ppermute(flow_u[:, :1, :], "gx", down_x)
    v_before = lax.ppermute(flow_v[:, :, rows_y - 1 :], "gy", up_y)
    v_after = lax.ppermute(flow_v[:, :, :1], "gy", down_y)
    u_next = jnp.concatenate([flow_u[:, 1:, :], u_after], axis=1)
    u_prev = jnp.concatenate([u_before, flow_u[:, :-1, :]], axis=1)
    v_next = jnp.concatenate([flow_v[:, :, 1:], v_after], axis=2)
    v_prev = jnp.concatenate([v_before, flow_v[:, :, :-1]], axis=2)
    diverge = ((u_next - u_prev) + (v_next - v_prev) + (raised(flow_w) - lowered(flow_w))) * 0.5

    total_y = rows_y * count_y
    n_q = 256
    n_p = total_y // n_q
    split_y = rows_y // n_q
    piece_x = rows_x // count_y
    sent = diverge.reshape(levels, count_y, piece_x, split_y, n_q).transpose(1, 3, 0, 2, 4)
    sent = sent.reshape(count_y, split_y * levels * piece_x, n_q)
    columns = lax.all_to_all(sent, "gy", split_axis=0, concat_axis=0, tiled=True)
    columns = columns.reshape(n_p, levels, piece_x, n_q)
    w1, t1c, t1s, w2 = y_tables(n_p, n_q)
    stage1 = lax.dot_general(
        const(w1), columns, (((1,), (0,)), ((), ())), precision=PREC
    )
    real1 = stage1[:n_p]
    imag1 = stage1[n_p:]
    tc = const(t1c)[:, None, None, :]
    ts = const(t1s)[:, None, None, :]
    real_t = real1 * tc + imag1 * ts
    imag_t = imag1 * tc - real1 * ts
    rows_m = levels * n_p * piece_x
    joined = jnp.concatenate(
        [real_t.reshape(rows_m, n_q), imag_t.reshape(rows_m, n_q)], axis=1
    )
    devices = count_x * count_y
    spectrum_y = lax.dot_general(
        const(w2.reshape(devices, 2, 2 * n_q)), joined, (((2,), (1,)), ((), ())), precision=PREC
    )
    moved = lax.all_to_all(spectrum_y, ("gx", "gy"), split_axis=0, concat_axis=0, tiled=True)

    total_x = rows_x * count_x
    n_s = devices
    n_i = piece_x
    scale = 1.0 / math.sqrt(total_x * total_y)
    wa, t2c, t2s, wb = x_tables(n_s, n_i, scale)
    stage_a = lax.dot_general(
        moved, const(wa.reshape(n_s, 2, 2 * n_s)), (((0, 1), (0, 1)), ((), ())), precision=PREC
    )
    batch = levels * n_p
    stage_a = stage_a.reshape(batch, n_i, 2 * n_s)
    real_a = stage_a[:, :, :n_s]
    imag_a = stage_a[:, :, n_s:]
    uc = const(t2c)[None]
    us = const(t2s)[None]
    real_b = real_a * uc + imag_a * us
    imag_b = imag_a * uc - real_a * us
    joined_x = jnp.concatenate([real_b, imag_b], axis=1)
    wbb = jnp.broadcast_to(const(wb)[None], (batch,) + wb.shape)
    result = lax.dot_general(
        wbb, joined_x, (((2,), (1,)), ((0,), (0,))), precision=PREC
    )
    result = result.reshape(n_p, levels, 2, n_i, n_s).transpose(2, 1, 0, 3, 4)
    spectrum = result.reshape(2, levels, n_p, total_x)
    return (tendency, spectrum)


def solution(mesh):
    return jax.shard_map(
        body,
        mesh=mesh,
        in_specs=(P(None, None, "gx", "gy"), P("gx", "gy"), P("gx", "gy")),
        out_specs=(P(None, None, "gx", "gy"), P(None, None, ("gx", "gy"), None)),
        check_vma=False,
    )
```

```python
import math

import numpy as np
import jax
import jax.numpy as jnp
from jax import lax
from jax.sharding import PartitionSpec as P


NU = 0.1
BETA = 0.5
HEAT = 1.0
DT = 0.5
PREC = lax.Precision.HIGH


def ring(count):
    up = [(i, (i + 1) % count) for i in range(count)]
    down = [(j, i) for i, j in up]
    return up, down


def raised(field):
    zero = jnp.zeros_like(field[:1])
    return jnp.concatenate([field[1:], zero], axis=0)


def lowered(field):
    zero = jnp.zeros_like(field[:1])
    return jnp.concatenate([zero, field[:-1]], axis=0)


def tendency_one(component, field, pick, center, fluid, surface):
    slope_x = (
        45.0 * (pick(1, 0) - pick(-1, 0))
        - 9.0 * (pick(2, 0) - pick(-2, 0))
        + (pick(3, 0) - pick(-3, 0))
    ) / 60.0
    slope_y = (
        45.0 * (pick(0, 1) - pick(0, -1))
        - 9.0 * (pick(0, 2) - pick(0, -2))
        + (pick(0, 3) - pick(0, -3))
    ) / 60.0
    above = raised(field)
    below = lowered(field)
    slope_z = (above - below) * 0.5
    advect = center[0] * slope_x + center[1] * slope_y + center[2] * slope_z
    spread = (
        pick(1, 0)
        + pick(-1, 0)
        + pick(0, 1)
        + pick(0, -1)
        - 4.0 * field
        + (above + below - 2.0 * field)
    )
    result = NU * spread - advect
    if component == 2:
        result = result + BETA * center[3]
    if component == 3:
        result = result + HEAT * surface
    return fluid * result


def cos_sin(rows, cols, length, scale=1.0):
    product = (np.arange(rows)[:, None] * np.arange(cols)[None, :]) % length
    angle = product * (2.0 * math.pi / length)
    return np.cos(angle) * scale, np.sin(angle) * scale


def const(array):
    return jnp.asarray(np.asarray(array, dtype=np.float32))


def y_tables(n_p, n_q):
    c1, s1 = cos_sin(n_p, n_p, n_p)
    w1 = np.concatenate([c1, -s1], axis=0)
    t_c, t_s = cos_sin(n_p, n_q, n_p * n_q)
    c2, s2 = cos_sin(n_q, n_q, n_q)
    w2 = np.zeros((n_q, 2, 2, n_q))
    w2[:, 0, 0] = c2
    w2[:, 0, 1] = s2
    w2[:, 1, 0] = -s2
    w2[:, 1, 1] = c2
    return w1, t_c, t_s, w2.reshape(2 * n_q, 2 * n_q)


def x_tables(n_s, n_i, scale):
    c2, s2 = cos_sin(n_s, n_s, n_s)
    wa = np.zeros((n_s, 2, 2, n_s))
    wa[:, 0, 0] = c2
    wa[:, 1, 0] = s2
    wa[:, 0, 1] = -s2
    wa[:, 1, 1] = c2
    t_c, t_s = cos_sin(n_i, n_s, n_s * n_i)
    cb, sb = cos_sin(n_i, n_i, n_i, scale)
    wb = np.zeros((2, n_i, 2, n_i))
    wb[0, :, 0] = cb
    wb[0, :, 1] = sb
    wb[1, :, 0] = -sb
    wb[1, :, 1] = cb
    return wa.reshape(2 * n_s, 2 * n_s), t_c, t_s, wb.reshape(2 * n_i, 2 * n_i)


def body(state, heights, surface_flag):
    levels = state.shape[1]
    rows_x = state.shape[2]
    rows_y = state.shape[3]
    count_x = lax.axis_size("gx")
    count_y = lax.axis_size("gy")
    up_x, down_x = ring(count_x)
    up_y, down_y = ring(count_y)

    level = lax.broadcasted_iota(jnp.int32, state.shape[1:], 0)
    fluid = (level >= heights[None]).astype(jnp.float32)
    surface = (level == heights[None]).astype(jnp.float32) * surface_flag[None].astype(jnp.float32)
    masked = state * fluid.astype(jnp.bfloat16)[None]

    def masked_part(xs, ys):
        lev = lax.broadcasted_iota(jnp.int32, (levels, xs.stop - xs.start, ys.stop - ys.start), 0)
        wet = (lev >= heights[None, xs, ys]).astype(jnp.bfloat16)
        return state[:, :, xs, ys] * wet[None]

    all_x, all_y = slice(0, rows_x), slice(0, rows_y)
    x_before = lax.ppermute(masked_part(slice(rows_x - 3, rows_x), all_y), "gx", up_x)
    x_after = lax.ppermute(masked_part(slice(0, 3), all_y), "gx", down_x)
    y_before = lax.ppermute(masked_part(all_x, slice(rows_y - 3, rows_y)), "gy", up_y)
    y_after = lax.ppermute(masked_part(all_x, slice(0, 3)), "gy", down_y)
    pad_x = jnp.concatenate([x_before, masked, x_after], axis=2).astype(jnp.float32)
    pad_y = jnp.concatenate([y_before, masked, y_after], axis=3).astype(jnp.float32)
    center = masked.astype(jnp.float32)

    pieces = []
    rounded = []
    for component in range(4):

        def pick(step_x, step_y, component=component):
            if step_y == 0:
                return pad_x[component, :, 3 + step_x : 3 + step_x + rows_x, :]
            return pad_y[component, :, :, 3 + step_y : 3 + step_y + rows_y]

        exact = tendency_one(component, center[component], pick, center, fluid, surface)
        pieces.append(exact.astype(jnp.bfloat16))
        rounded.append(lax.reduce_precision(exact, exponent_bits=8, mantissa_bits=7))
    tendency = jnp.stack(pieces)

    flows = []
    for component in range(3):
        flows.append(center[component] + DT * rounded[component])
    flow_u, flow_v, flow_w = flows
    u_before = lax.ppermute(flow_u[:, rows_x - 1 :, :], "gx", up_x)
    u_after = lax.ppermute(flow_u[:, :1, :], "gx", down_x)
    v_before = lax.ppermute(flow_v[:, :, rows_y - 1 :], "gy", up_y)
    v_after = lax.ppermute(flow_v[:, :, :1], "gy", down_y)
    u_next = jnp.concatenate([flow_u[:, 1:, :], u_after], axis=1)
    u_prev = jnp.concatenate([u_before, flow_u[:, :-1, :]], axis=1)
    v_next = jnp.concatenate([flow_v[:, :, 1:], v_after], axis=2)
    v_prev = jnp.concatenate([v_before, flow_v[:, :, :-1]], axis=2)
    diverge = ((u_next - u_prev) + (v_next - v_prev) + (raised(flow_w) - lowered(flow_w))) * 0.5

    total_y = rows_y * count_y
    n_q = 256
    n_p = total_y // n_q
    split_y = rows_y // n_q
    piece_x = rows_x // count_y
    sent = diverge.reshape(levels, count_y, piece_x, split_y, n_q).transpose(1, 3, 0, 2, 4)
    sent = sent.reshape(count_y, split_y * levels * piece_x, n_q)
    columns = lax.all_to_all(sent, "gy", split_axis=0, concat_axis=0, tiled=True)
    columns = columns.reshape(n_p, levels * piece_x, n_q)
    w1, t1c, t1s, w2 = y_tables(n_p, n_q)
    stage1 = lax.dot_general(
        const(w1), columns, (((1,), (0,)), ((), ())), precision=PREC
    )
    real1 = stage1[:n_p]
    imag1 = stage1[n_p:]
    tc = const(t1c)[:, None, :]
    ts = const(t1s)[:, None, :]
    real_t = real1 * tc + imag1 * ts
    imag_t = imag1 * tc - real1 * ts
    rows_m = levels * n_p * piece_x
    joined = jnp.concatenate(
        [real_t.reshape(rows_m, n_q), imag_t.reshape(rows_m, n_q)], axis=1
    )
    devices = count_x * count_y
    spectrum_y = lax.dot_general(
        const(w2.reshape(devices, 2, 2 * n_q)), joined, (((2,), (1,)), ((), ())), precision=PREC
    )
    moved = lax.all_to_all(spectrum_y, ("gx", "gy"), split_axis=0, concat_axis=0, tiled=True)

    total_x = rows_x * count_x
    n_s = devices
    n_i = piece_x
    scale = 1.0 / math.sqrt(total_x * total_y)
    wa, t2c, t2s, wb = x_tables(n_s, n_i, scale)
    stage_a = lax.dot_general(
        moved, const(wa.reshape(n_s, 2, 2 * n_s)), (((0, 1), (0, 1)), ((), ())), precision=PREC
    )
    batch = levels * n_p
    stage_a = stage_a.reshape(batch, n_i, 2 * n_s)
    real_a = stage_a[:, :, :n_s]
    imag_a = stage_a[:, :, n_s:]
    uc = const(t2c)[None]
    us = const(t2s)[None]
    real_b = real_a * uc + imag_a * us
    imag_b = imag_a * uc - real_a * us
    joined_x = jnp.concatenate([real_b, imag_b], axis=1)
    wbb = jnp.broadcast_to(const(wb)[None], (batch,) + wb.shape)
    result = lax.dot_general(
        wbb, joined_x, (((2,), (1,)), ((0,), (0,))), precision=PREC
    )
    result = result.reshape(n_p, levels, 2, n_i, n_s).transpose(2, 1, 0, 3, 4)
    spectrum = result.reshape(2, levels, n_p, total_x)
    return (tendency, spectrum)


def solution(mesh):
    return jax.shard_map(
        body,
        mesh=mesh,
        in_specs=(P(None, None, "gx", "gy"), P("gx", "gy"), P("gx", "gy")),
        out_specs=(P(None, None, "gx", "gy"), P(None, None, ("gx", "gy"), None)),
        check_vma=False,
    )
```
